256 devices in a mesh: gx: 8 (over x, z_hi), gy: 4 (over z_lo), gz: 8 (over y, core).
Axes of the slice: x: 4, y: 4, z: 8 (z_hi: 2, z_lo: 4; z = z_hi * 4 + z_lo), core: 2. Of those that a mesh axis runs over, the one named last changes fastest.
Arguments:
- plus_blocks: float32 [8, 4, 8, 3, 4, 256, 256], P('gx', 'gy', 'gz'), may hold values from -0.1 to 4, as said below
- minus_blocks: float32 [8, 4, 8, 3, 4, 256, 256], P('gx', 'gy', 'gz'), may hold values from -0.1 to 4, as said below
- inner_blocks: float32 [8, 4, 8, 2, 8, 256, 256], P('gx', 'gy', 'gz'), may hold values from -0.1 to 4, as said below
- initial_subspace: float32 [8, 4, 8, 20, 16, 256], P('gx', 'gy', 'gz'), may hold values from -6 to 6
- picks: int32 [8, 4, 8, 20, 8], P('gx', 'gy', 'gz'), may hold values from 0 to 15, all different within a row
- owner: int32 [8, 4, 8, 20], P('gx', 'gy', 'gz'), may hold values from 0 to 127
- material_class: int32 [8, 4, 8], P('gx', 'gy', 'gz'), may hold values from 0 to 3
- coef: float32 [4], replicated, may hold values from 1 to 4
Outputs:
- constraints: float32 [8, 4, 8, 20, 8, 256], P('gx', 'gy', 'gz')
- coarse: float32 [8, 4, 128, 64], P('gx', 'gy', 'gz')
The draws below stay inside these ranges and needn't reach their ends.
Inputs may be any that keep to these rules, and one draw needn't show every extreme that they name: Each face's picks are distinct. `plus_blocks`: symmetric blocks, diagonal entries from 1 to 4, off-diagonal entries within -0.1 to 0.1. `minus_blocks`: symmetric blocks, diagonal entries from 1 to 4, off-diagonal entries within -0.1 to 0.1. `inner_blocks`: symmetric blocks, diagonal entries from 1 to 4, off-diagonal entries within -0.1 to 0.1.
All inputs are finite; a program needn't handle non-finite values.
Results may differ from the reference program's by a relative error of at most 0.00012.
Values sent between devices are 32-bit elements; how exact they have to be, the bound alone decides.
No kernel may reach another device: no remote copies, remote signals or barrier semaphores. Data moves between devices by JAX's collectives and lax.ppermute only.
A program may use at most 128 MiB of HBM per device.

```python
import math
import jax
import jax.numpy as jnp
from jax import lax

F = 256
NV = 16
NSEL = 8
ITERS = 4
NCLASS = 4
CROSS = 4
INNER = 8
GX = 8
GY = 4
GZ = 8
FACES = 20
ROWS = 128


def block_draw(key, shape):
    first, second = jax.random.split(key, 2)
    size = shape[-1]
    raw = jax.random.truncated_normal(first, -4.0, 4.0, shape, jnp.float32)
    offdiag = (raw + jnp.swapaxes(raw, -1, -2)) * (0.35 / math.sqrt(2.0 * size))
    offdiag = jnp.clip(offdiag, -0.1, 0.1)
    diagonal = jnp.exp(jax.random.uniform(second, shape[:-1], jnp.float32, math.log(1.0), math.log(4.0)))
    identity = jnp.eye(size, dtype=jnp.float32)
    return offdiag * (1.0 - identity) + identity * diagonal[..., None]


def draw_plus_blocks(key, part):
    return block_draw(jax.random.fold_in(key, 11), (GX, GY, GZ, 3, CROSS, F, F))


def draw_minus_blocks(key, part):
    return block_draw(jax.random.fold_in(key, 23), (GX, GY, GZ, 3, CROSS, F, F))


def draw_inner_blocks(key, part):
    return block_draw(jax.random.fold_in(key, 37), (GX, GY, GZ, 2, INNER, F, F))


def plant(drawn, rng, least, high):
    dims = drawn.shape
    place = [jax.random.randint(jax.random.fold_in(rng, axis), (), 0, dims[axis]) for axis in range(len(dims))]
    drawn = drawn.at[tuple(place)].set(least)
    longest = dims.index(max(dims))
    place[longest] = (place[longest] + 1) % dims[longest]
    return drawn.at[tuple(place)].set(high)


def shard_levels(stream_key, dims, shards, low, high):
    loudness, own = 1.0, jax.random.fold_in(stream_key, 6)
    for position, blocks in shards:
        steps = jnp.exp(jax.random.uniform(jax.random.fold_in(own, position), (blocks,), jnp.float32, low / len(shards), high / len(shards)))
        loudness = loudness * jnp.repeat(steps, dims[position] // blocks).reshape([-1 if axis == position else 1 for axis in range(len(dims))])
    return loudness


def different_ones(stream_key, rows, number_of, top, lift):
    order = jax.random.permutation(jax.random.fold_in(stream_key, 1), number_of)
    boost = order
    for power in range(3):
        boost = boost * boost // number_of
    boost = boost * lift // number_of
    tickets = jax.random.randint(jax.random.fold_in(stream_key, 2), (rows, number_of), 0, 4096) + boost
    fixed_rows = jax.random.permutation(jax.random.fold_in(stream_key, 3), rows)[jnp.arange(number_of) % rows]
    tickets = jnp.where(jnp.arange(rows)[:, None] == fixed_rows[None, :], 1 << 14, tickets)
    priority = tickets * number_of + jnp.arange(number_of)
    return lax.top_k(priority.astype(jnp.int32), top)[1].astype(jnp.int32)


def bell_draw(key, shape, width, reach, pieces=(), kind=jnp.bfloat16):
    result = width * jax.random.normal(key, shape, jnp.float32)
    if pieces:
        result = result * shard_levels(key, shape, pieces, -0.22, 0.18)
    return jnp.clip(result, -reach, reach).astype(kind)


def setup_inputs(seed: int = 0) -> dict:
    keys = jax.random.split(jax.random.key(seed), 9)
    plus_blocks = draw_plus_blocks(jax.random.fold_in(keys[8], 71), 0)
    minus_blocks = draw_minus_blocks(jax.random.fold_in(keys[8], 71), 0)
    inner_blocks = draw_inner_blocks(jax.random.fold_in(keys[8], 71), 0)
    initial_subspace = bell_draw(keys[3], (GX, GY, GZ, FACES, NV, F), 1.0, 6.0, ((0, 8), (1, 4), (2, 8)), jnp.float32)
    picks = different_ones(keys[4], GX * GY * GZ * FACES, NV, NSEL, 0).reshape((GX, GY, GZ, FACES, NSEL))
    owner = plant(jax.random.randint(keys[5], (GX, GY, GZ, FACES), 0, ROWS), jax.random.fold_in(keys[5], 1), 0, ROWS - 1).astype(jnp.int32)
    material_class = plant(jax.random.randint(keys[6], (GX, GY, GZ), 0, NCLASS), jax.random.fold_in(keys[6], 1), 0, NCLASS - 1).astype(jnp.int32)
    coef = jnp.clip(jnp.exp(jax.random.uniform(keys[7], (NCLASS,), jnp.float32, math.log(1.0), math.log(4.0))), 1.0, 4.0)
    return dict(plus_blocks=plus_blocks, minus_blocks=minus_blocks, inner_blocks=inner_blocks, initial_subspace=initial_subspace, picks=picks, owner=owner, material_class=material_class, coef=coef)


def following_shift(values, axis):
    rest = lax.slice_in_dim(values, 1, values.shape[axis], axis=axis)
    zeros = jnp.zeros_like(lax.slice_in_dim(values, 0, 1, axis=axis))
    return jnp.concatenate([rest, zeros], axis=axis)

def subspace(matrices, basis_vectors):
    largest_eigen = lax.Precision.HIGHEST
    for iteration in range(ITERS):
        images = jnp.einsum('bkg,bfg->bkf', basis_vectors, matrices, precision=largest_eigen)
        gram_matrix = jnp.einsum('bkg,bjg->bkj', images, images, precision=largest_eigen)
        lower_tri = jnp.linalg.cholesky(gram_matrix)
        basis_vectors = jax.scipy.linalg.solve_triangular(lower_tri, images, lower=True)
    return basis_vectors

def reference(plus_blocks, minus_blocks, inner_blocks, initial_subspace, picks, owner, material_class, coef):
    largest_eigen = lax.Precision.HIGHEST
    scale = jnp.take(coef, material_class)
    wide = scale[:, :, :, None, None, None]
    crossing = []
    for axis in range(3):
        partner = following_shift(wide * minus_blocks[:, :, :, axis], axis)
        crossing.append(wide * plus_blocks[:, :, :, axis] + partner)
    cross_mats = jnp.stack(crossing, axis=3)
    shape = cross_mats.shape
    cross_mats = cross_mats.reshape(shape[0], shape[1], shape[2], 3 * shape[4], F, F)
    inner_mats = wide * inner_blocks[:, :, :, 0] + wide * inner_blocks[:, :, :, 1]
    matrices = jnp.concatenate([cross_mats, inner_mats], axis=3)
    lead = matrices.shape[:4]
    flat_mats = matrices.reshape(-1, F, F)
    basis_vectors = subspace(flat_mats, initial_subspace.reshape(-1, NV, F))
    indicator_rows = (picks.reshape(-1, NSEL)[:, :, None] == jnp.arange(NV, dtype=jnp.int32)).astype(jnp.float32)
    picked_modes = jnp.einsum('iow,iwh->ioh', indicator_rows, basis_vectors, precision=largest_eigen)
    images = jnp.einsum('btg,bfg->btf', picked_modes, flat_mats, precision=largest_eigen)
    blocks = jnp.einsum('bsd,btd->bst', picked_modes, images, precision=largest_eigen)
    blocks = blocks.reshape(lead + (NSEL * NSEL,)) / scale[:, :, :, None, None]
    owner_hot = (owner[..., None] == jnp.arange(ROWS, dtype=jnp.int32)).astype(jnp.float32)
    coarse = jnp.einsum('xyzfr,xyzfe->xyre', owner_hot, blocks, precision=largest_eigen)
    constraints = (picked_modes * math.sqrt(F)).reshape(lead + (NSEL, F))
    return (constraints, coarse)
```

```python
import functools
import math

import jax
import jax.numpy as jnp
from jax import lax
from jax.experimental import pallas as pl
from jax.experimental.pallas import tpu as pltpu
from jax.sharding import PartitionSpec as P

ITERS = 4
CROWS = 16
HIGHEST = lax.Precision.HIGHEST


def passed_along(block, axis, distance):
    devices = range(lax.axis_size(axis))
    route = [(i - distance, i) for i in devices if i - distance in devices]
    return lax.ppermute(block, axis, route)


def eliminate(gram):
    faces, count, _ = gram.shape
    sub = lax.broadcasted_iota(jnp.int32, (faces, count, count), 1)
    lane = lax.broadcasted_iota(jnp.int32, (faces, count, count), 2)
    left = gram
    right = (sub == lane).astype(jnp.float32)
    for j in range(count):
        row_l = jnp.sum(jnp.where(sub == j, left, 0.0), axis=1, keepdims=True)
        row_r = jnp.sum(jnp.where(sub == j, right, 0.0), axis=1, keepdims=True)
        pivot = jnp.sum(jnp.where(lane[:, :1] == j, row_l, 0.0), axis=2, keepdims=True)
        inv = 1.0 / jnp.sqrt(pivot)
        col = jnp.sum(jnp.where(lane == j, left, 0.0), axis=2, keepdims=True) * inv
        col = jnp.where(sub[:, :, :1] > j, col, 0.0)
        row_l = row_l * inv
        row_r = row_r * inv
        left = jnp.where(sub == j, row_l, left - col * row_l)
        right = jnp.where(sub == j, row_r, right - col * row_r)
    return right


def face_kernel(scal_ref, picks_ref, a_ref, b_ref, v0_ref, c_ref, e_ref, m_scr, v_scr, w_scr, g_scr):
    faces = a_ref.shape[0]
    nsel = c_ref.shape[1]
    own = scal_ref[0]

    def build(f, carry):
        m_scr[f] = own * a_ref[f] + scal_ref[1 + f] * b_ref[f]
        v_scr[f] = v0_ref[f]
        return carry

    lax.fori_loop(0, faces, build, 0)

    def image(f, carry):
        w = jnp.dot(v_scr[f], m_scr[f], precision=HIGHEST, preferred_element_type=jnp.float32)
        w_scr[f] = w
        g_scr[f] = lax.dot_general(
            w, w, (((1,), (1,)), ((), ())), precision=HIGHEST, preferred_element_type=jnp.float32
        )
        return carry

    def solve(f, carry):
        v_scr[f] = jnp.dot(g_scr[f], w_scr[f], precision=HIGHEST, preferred_element_type=jnp.float32)
        return carry

    for iteration in range(ITERS):
        lax.fori_loop(0, faces, image, 0)
        g_scr[...] = eliminate(g_scr[...])
        lax.fori_loop(0, faces, solve, 0)

    def finish(f, carry):
        rows = [v_scr[f, pl.ds(picks_ref[f * nsel + s], 1), :] for s in range(nsel)]
        picked = jnp.concatenate(rows, axis=0)
        c_ref[f] = picked
        images = jnp.dot(picked, m_scr[f], precision=HIGHEST, preferred_element_type=jnp.float32)
        block = lax.dot_general(
            picked, images, (((1,), (1,)), ((), ())), precision=HIGHEST, preferred_element_type=jnp.float32
        )
        e_ref[f] = block / own
        return carry

    lax.fori_loop(0, faces, finish, 0)


def run_faces(scalars, picks, first, second, start):
    faces, width = first.shape[0], first.shape[-1]
    count = start.shape[1]
    nsel = picks.shape[1]
    vmem = pltpu.MemorySpace.VMEM
    smem = pltpu.MemorySpace.SMEM
    return pl.pallas_call(
        face_kernel,
        out_shape=(
            jax.ShapeDtypeStruct((faces, nsel, width), jnp.float32),
            jax.ShapeDtypeStruct((faces, nsel, nsel), jnp.float32),
        ),
        in_specs=[
            pl.BlockSpec(memory_space=smem),
            pl.BlockSpec(memory_space=smem),
            pl.BlockSpec(memory_space=vmem),
            pl.BlockSpec(memory_space=vmem),
            pl.BlockSpec(memory_space=vmem),
        ],
        out_specs=(pl.BlockSpec(memory_space=vmem), pl.BlockSpec(memory_space=vmem)),
        scratch_shapes=[
            pltpu.VMEM((faces, width, width), jnp.float32),
            pltpu.VMEM((faces, count, width), jnp.float32),
            pltpu.VMEM((faces, count, width), jnp.float32),
            pltpu.VMEM((faces, count, count), jnp.float32),
        ],
        compiler_params=pltpu.CompilerParams(vmem_limit_bytes=60 * 1024 * 1024),
    )(scalars, picks.reshape(-1), first, second, start)


def per_device(
    plus_blocks, minus_blocks, inner_blocks, initial_subspace, picks, owner, material_class, coef
):
    plus_local = plus_blocks[0, 0, 0]
    minus_local = minus_blocks[0, 0, 0]
    inner_local = inner_blocks[0, 0, 0]
    basis_vectors = initial_subspace[0, 0, 0]
    picks_local = picks[0, 0, 0]
    dims, crossing, width = plus_local.shape[0], plus_local.shape[1], plus_local.shape[-1]
    matches = material_class.reshape(()) == jnp.arange(coef.shape[0], dtype=jnp.int32)
    own_scale = jnp.sum(jnp.where(matches, coef, 0.0))
    axes = ("gx", "gy", "gz")
    partners = [passed_along(minus_local[a], axes[a], -1) for a in range(dims)]
    next_scales = [passed_along(own_scale, axes[a], -1) for a in range(dims)]

    n_inner = inner_local.shape[1]
    inner_scal = jnp.full((1 + n_inner,), own_scale, jnp.float32)
    inner_c, inner_e = run_faces(
        inner_scal, picks_local[dims * crossing :], inner_local[0], inner_local[1],
        basis_vectors[dims * crossing :],
    )
    cross_scal = jnp.concatenate(
        [own_scale[None]] + [jnp.broadcast_to(s, (crossing,)) for s in next_scales]
    )
    cross_c, cross_e = run_faces(
        cross_scal, picks_local[: dims * crossing], plus_local.reshape(dims * crossing, width, width),
        jnp.stack(partners).reshape(dims * crossing, width, width), basis_vectors[: dims * crossing],
    )
    picked_modes = jnp.concatenate([cross_c, inner_c], axis=0)
    blocks = jnp.concatenate([cross_e, inner_e], axis=0)
    faces = blocks.shape[0]
    flat = blocks.reshape(faces, -1)
    groups = lax.axis_size("gz")
    rows_all = groups * CROWS
    owner_hot = (owner[0, 0, 0][:, None] == jnp.arange(rows_all, dtype=jnp.int32)).astype(jnp.float32)
    term = jnp.einsum("fr,fe->re", owner_hot, flat, precision=HIGHEST).reshape(groups, CROWS, -1)
    me = lax.axis_index("gz")
    coarse = term[me]
    for shift in range(1, groups):
        part = lax.dynamic_index_in_dim(term, (me + shift) % groups, 0, keepdims=False)
        route = [(i, (i + shift) % groups) for i in range(groups)]
        coarse = coarse + lax.ppermute(part, "gz", route)
    constraints = picked_modes * math.sqrt(width)
    return (constraints[None, None, None], coarse[None, None])


def solution(mesh):
    return jax.shard_map(
        per_device,
        mesh=mesh,
        in_specs=(
            P("gx", "gy", "gz", None, None, None, None),
            P("gx", "gy", "gz", None, None, None, None),
            P("gx", "gy", "gz", None, None, None, None),
            P("gx", "gy", "gz", None, None, None),
            P("gx", "gy", "gz", None, None),
            P("gx", "gy", "gz", None),
            P("gx", "gy", "gz"),
            P(),
        ),
        out_specs=(P("gx", "gy", "gz", None, None, None), P("gx", "gy", "gz", None)),
        check_vma=False,
    )
```

```python
import math

import jax
import jax.numpy as jnp
from jax import lax
from jax.experimental import pallas as pl
from jax.experimental.pallas import tpu as pltpu
from jax.sharding import PartitionSpec as P

ITERS = 4
CROWS = 16
HIGHEST = lax.Precision.HIGHEST


def passed_along(block, axis, distance):
    devices = range(lax.axis_size(axis))
    route = [(i - distance, i) for i in devices if i - distance in devices]
    return lax.ppermute(block, axis, route)


def eliminate(gram):
    faces, count, _ = gram.shape
    sub = lax.broadcasted_iota(jnp.int32, (faces, count, count), 1)
    lane = lax.broadcasted_iota(jnp.int32, (faces, count, count), 2)
    left = gram
    right = (sub == lane).astype(jnp.float32)
    for j in range(count):
        row_l = jnp.sum(jnp.where(sub == j, left, 0.0), axis=1, keepdims=True)
        row_r = jnp.sum(jnp.where(sub == j, right, 0.0), axis=1, keepdims=True)
        pivot = jnp.sum(jnp.where(lane[:, :1] == j, row_l, 0.0), axis=2, keepdims=True)
        inv = 1.0 / jnp.sqrt(pivot)
        col = jnp.sum(jnp.where(lane == j, left, 0.0), axis=2, keepdims=True) * inv
        col = jnp.where(sub[:, :, :1] > j, col, 0.0)
        row_l = row_l * inv
        row_r = row_r * inv
        left = jnp.where(sub == j, row_l, left - col * row_l)
        right = jnp.where(sub == j, row_r, right - col * row_r)
    return right


def iterate(own, picks_ref, pick_base, c_ref, e_ref, m_scr, v_scr, w_scr, g_scr):
    faces = m_scr.shape[0]
    nsel = c_ref.shape[1]
    scale_out = math.sqrt(m_scr.shape[-1])

    def image(f, carry):
        w = jnp.dot(v_scr[f], m_scr[f], precision=HIGHEST, preferred_element_type=jnp.float32)
        w_scr[f] = w
        g_scr[f] = lax.dot_general(
            w, w, (((1,), (1,)), ((), ())), precision=HIGHEST, preferred_element_type=jnp.float32
        )
        return carry

    def solve(f, carry):
        v_scr[f] = jnp.dot(g_scr[f], w_scr[f], precision=HIGHEST, preferred_element_type=jnp.float32)
        return carry

    for iteration in range(ITERS):
        lax.fori_loop(0, faces, image, 0, unroll=4)
        g_scr[...] = eliminate(g_scr[...])
        lax.fori_loop(0, faces, solve, 0, unroll=4)

    def finish(f, carry):
        rows = [v_scr[f, pl.ds(picks_ref[pick_base + f * nsel + s], 1), :] for s in range(nsel)]
        picked = jnp.concatenate(rows, axis=0)
        c_ref[f] = picked * scale_out
        images = jnp.dot(picked, m_scr[f], precision=HIGHEST, preferred_element_type=jnp.float32)
        block = lax.dot_general(
            picked, images, (((1,), (1,)), ((), ())), precision=HIGHEST, preferred_element_type=jnp.float32
        )
        e_ref[f] = block / own
        return carry

    lax.fori_loop(0, faces, finish, 0, unroll=2)


def inner_kernel(scal_ref, picks_ref, inner_ref, v0_ref, c_ref, e_ref, m_scr, v_scr, w_scr, g_scr):
    faces = m_scr.shape[0]
    base = v0_ref.shape[0] - faces
    own = scal_ref[0]
    for f in range(faces):
        m_scr[f] = own * inner_ref[0, f] + own * inner_ref[1, f]
        v_scr[f] = v0_ref[base + f]
    iterate(own, picks_ref, base * c_ref.shape[1], c_ref, e_ref, m_scr, v_scr, w_scr, g_scr)


def unpacked(packed, side, index, pairs):
    width = packed.shape[-1]
    row = lax.broadcasted_iota(jnp.int32, (width, width), 0)
    col = lax.broadcasted_iota(jnp.int32, (width, width), 1)
    mixed = packed[index % pairs]
    turned = mixed.T
    if index < pairs:
        return jnp.where(col >= row, mixed, turned)
    diagonal = side[index - pairs : index - pairs + 1, :]
    return jnp.where(col > row, turned, jnp.where(col == row, diagonal, mixed))


def cross_kernel(scal_ref, picks_ref, plus_ref, *refs):
    dims = plus_ref.shape[0]
    packed_refs = refs[:dims]
    side_refs = refs[dims : 2 * dims]
    v0_ref, c_ref, e_ref, m_scr, v_scr, w_scr, g_scr = refs[2 * dims :]
    crossing = plus_ref.shape[1]
    pairs = packed_refs[0].shape[0]
    own = scal_ref[0]
    for a in range(dims):
        side = side_refs[a][...]
        packed = packed_refs[a]
        next_scale = side[pairs : pairs + 1, 0:1]
        for k in range(crossing):
            f = a * crossing + k
            m_scr[f] = own * plus_ref[a, k] + next_scale * unpacked(packed, side, k, pairs)
            v_scr[f] = v0_ref[f]
    iterate(own, picks_ref, 0, c_ref, e_ref, m_scr, v_scr, w_scr, g_scr)


def run_faces(kernel, faces, nsel, width, count, smem_args, vmem_args):
    vmem = pltpu.MemorySpace.VMEM
    smem = pltpu.MemorySpace.SMEM
    return pl.pallas_call(
        kernel,
        out_shape=(
            jax.ShapeDtypeStruct((faces, nsel, width), jnp.float32),
            jax.ShapeDtypeStruct((faces, nsel, nsel), jnp.float32),
        ),
        in_specs=[pl.BlockSpec(memory_space=smem)] * len(smem_args)
        + [pl.BlockSpec(memory_space=vmem)] * len(vmem_args),
        out_specs=(pl.BlockSpec(memory_space=vmem), pl.BlockSpec(memory_space=vmem)),
        scratch_shapes=[
            pltpu.VMEM((faces, width, width), jnp.float32),
            pltpu.VMEM((faces, count, width), jnp.float32),
            pltpu.VMEM((faces, count, width), jnp.float32),
            pltpu.VMEM((faces, count, count), jnp.float32),
        ],
        compiler_params=pltpu.CompilerParams(vmem_limit_bytes=60 * 1024 * 1024),
    )(*smem_args, *vmem_args)


def per_device(
    plus_blocks, minus_blocks, inner_blocks, initial_subspace, picks, owner, material_class, coef
):
    plus_local = plus_blocks[0, 0, 0]
    minus_local = minus_blocks[0, 0, 0]
    inner_local = inner_blocks[0, 0, 0]
    basis_vectors = initial_subspace[0, 0, 0]
    picks_flat = picks[0, 0, 0].reshape(-1)
    dims, crossing, width = plus_local.shape[0], plus_local.shape[1], plus_local.shape[-1]
    faces_all, count = basis_vectors.shape[0], basis_vectors.shape[1]
    nsel = picks.shape[-1]
    pairs = crossing // 2
    matches = material_class.reshape(()) == jnp.arange(coef.shape[0], dtype=jnp.int32)
    own_scale = jnp.sum(jnp.where(matches, coef, 0.0))
    row = lax.broadcasted_iota(jnp.int32, (width, width), 0)
    col = lax.broadcasted_iota(jnp.int32, (width, width), 1)
    axes = ("gx", "gy", "gz")
    packed_in = []
    side_in = []
    for a in range(dims):
        halves = minus_local[a]
        packed = jnp.where(col >= row, halves[:pairs], halves[pairs:])
        diagonals = jnp.diagonal(halves[pairs:], axis1=1, axis2=2)
        side = jnp.concatenate([diagonals, jnp.broadcast_to(own_scale, (1, width))], axis=0)
        packed_in.append(passed_along(packed, axes[a], -1))
        side_in.append(passed_along(side, axes[a], -1))

    scal = own_scale.reshape(1)
    n_inner = inner_local.shape[1]
    inner_c, inner_e = run_faces(
        inner_kernel, n_inner, nsel, width, count, (scal, picks_flat), (inner_local, basis_vectors)
    )
    cross_c, cross_e = run_faces(
        cross_kernel, dims * crossing, nsel, width, count, (scal, picks_flat),
        (plus_local, *packed_in, *side_in, basis_vectors),
    )
    constraints = jnp.concatenate([cross_c, inner_c], axis=0)
    blocks = jnp.concatenate([cross_e, inner_e], axis=0)
    flat = blocks.reshape(faces_all, -1)
    groups = lax.axis_size("gz")
    rows_all = groups * CROWS
    owner_hot = (owner[0, 0, 0][:, None] == jnp.arange(rows_all, dtype=jnp.int32)).astype(jnp.float32)
    term = jnp.einsum("fr,fe->re", owner_hot, flat, precision=HIGHEST).reshape(groups, CROWS, -1)
    me = lax.axis_index("gz")
    coarse = lax.dynamic_index_in_dim(term, me, 0, keepdims=False)
    for shift in range(1, groups):
        part = lax.dynamic_index_in_dim(term, (me + shift) % groups, 0, keepdims=False)
        route = [(i, (i + shift) % groups) for i in range(groups)]
        coarse = coarse + lax.ppermute(part, "gz", route)
    return (constraints[None, None, None], coarse[None, None])


def solution(mesh):
    return jax.shard_map(
        per_device,
        mesh=mesh,
        in_specs=(
            P("gx", "gy", "gz", None, None, None, None),
            P("gx", "gy", "gz", None, None, None, None),
            P("gx", "gy", "gz", None, None, None, None),
            P("gx", "gy", "gz", None, None, None),
            P("gx", "gy", "gz", None, None),
            P("gx", "gy", "gz", None),
            P("gx", "gy", "gz"),
            P(),
        ),
        out_specs=(P("gx", "gy", "gz", None, None, None), P("gx", "gy", "gz", None)),
        check_vma=False,
    )
```

```python
import math

import jax
import jax.numpy as jnp
from jax import lax
from jax.experimental import pallas as pl
from jax.experimental.pallas import tpu as pltpu
from jax.sharding import PartitionSpec as P

ITERS = 4
CROWS = 16
HIGHEST = lax.Precision.HIGHEST


def passed_along(block, axis, distance):
    devices = range(lax.axis_size(axis))
    route = [(i - distance, i) for i in devices if i - distance in devices]
    return lax.ppermute(block, axis, route)


def eliminate(gram):
    faces, count, _ = gram.shape
    sub = lax.broadcasted_iota(jnp.int32, (faces, count, count), 1)
    lane = lax.broadcasted_iota(jnp.int32, (faces, count, count), 2)
    left = gram
    right = (sub == lane).astype(jnp.float32)
    for j in range(count):
        row_l = jnp.sum(jnp.where(sub == j, left, 0.0), axis=1, keepdims=True)
        row_r = jnp.sum(jnp.where(sub == j, right, 0.0), axis=1, keepdims=True)
        pivot = jnp.sum(jnp.where(lane[:, :1] == j, row_l, 0.0), axis=2, keepdims=True)
        inv = 1.0 / jnp.sqrt(pivot)
        col = jnp.sum(jnp.where(lane == j, left, 0.0), axis=2, keepdims=True) * inv
        col = jnp.where(sub[:, :, :1] > j, col, 0.0)
        row_l = row_l * inv
        row_r = row_r * inv
        left = jnp.where(sub == j, row_l, left - col * row_l)
        right = jnp.where(sub == j, row_r, right - col * row_r)
    return right


def iterate(own, picks_ref, pick_base, c_ref, e_ref, m_scr, v_scr, w_scr, g_scr):
    faces = m_scr.shape[0]
    nsel = c_ref.shape[1]
    scale_out = math.sqrt(m_scr.shape[-1])

    def image(f, carry):
        w = jnp.dot(v_scr[f], m_scr[f], precision=HIGHEST, preferred_element_type=jnp.float32)
        w_scr[f] = w
        g_scr[f] = lax.dot_general(
            w, w, (((1,), (1,)), ((), ())), precision=HIGHEST, preferred_element_type=jnp.float32
        )
        return carry

    def solve(f, carry):
        v_scr[f] = jnp.dot(g_scr[f], w_scr[f], precision=HIGHEST, preferred_element_type=jnp.float32)
        return carry

    for iteration in range(ITERS):
        lax.fori_loop(0, faces, image, 0, unroll=4)
        g_scr[...] = eliminate(g_scr[...])
        lax.fori_loop(0, faces, solve, 0, unroll=4)

    def finish(f, carry):
        rows = [v_scr[f, pl.ds(picks_ref[pick_base + f * nsel + s], 1), :] for s in range(nsel)]
        picked = jnp.concatenate(rows, axis=0)
        c_ref[f] = picked * scale_out
        images = jnp.dot(picked, m_scr[f], precision=HIGHEST, preferred_element_type=jnp.float32)
        block = lax.dot_general(
            picked, images, (((1,), (1,)), ((), ())), precision=HIGHEST, preferred_element_type=jnp.float32
        )
        e_ref[f] = block / own
        return carry

    lax.fori_loop(0, faces, finish, 0, unroll=2)


def inner_kernel(scal_ref, picks_ref, inner_ref, v0_ref, c_ref, e_ref, m_scr, v_scr, w_scr, g_scr):
    faces = m_scr.shape[0]
    base = v0_ref.shape[0] - faces
    own = scal_ref[0]
    for f in range(faces):
        m_scr[f] = own * inner_ref[0, f] + own * inner_ref[1, f]
        v_scr[f] = v0_ref[base + f]
    iterate(own, picks_ref, base * c_ref.shape[1], c_ref, e_ref, m_scr, v_scr, w_scr, g_scr)


def unpacked(packed, side, index, pairs):
    width = packed.shape[-1]
    row = lax.broadcasted_iota(jnp.int32, (width, width), 0)
    col = lax.broadcasted_iota(jnp.int32, (width, width), 1)
    mixed = packed[index % pairs]
    turned = mixed.T
    if index < pairs:
        return jnp.where(col >= row, mixed, turned)
    diagonal = side[index - pairs : index - pairs + 1, :]
    return jnp.where(col > row, turned, jnp.where(col == row, diagonal, mixed))


def cross_kernel(scal_ref, picks_ref, plus_ref, *refs):
    dims = plus_ref.shape[0]
    packed_refs = refs[:dims]
    side_refs = refs[dims : 2 * dims]
    v0_ref, c_ref, e_ref, m_scr, v_scr, w_scr, g_scr = refs[2 * dims :]
    crossing = plus_ref.shape[1]
    pairs = packed_refs[0].shape[0]
    own = scal_ref[0]
    for a in range(dims):
        side = side_refs[a][...]
        packed = packed_refs[a]
        next_scale = side[pairs : pairs + 1, 0:1]
        for k in range(crossing):
            f = a * crossing + k
            m_scr[f] = own * plus_ref[a, k] + next_scale * unpacked(packed, side, k, pairs)
            v_scr[f] = v0_ref[f]
    iterate(own, picks_ref, 0, c_ref, e_ref, m_scr, v_scr, w_scr, g_scr)


def run_faces(kernel, faces, nsel, width, count, smem_args, vmem_args):
    vmem = pltpu.MemorySpace.VMEM
    smem = pltpu.MemorySpace.SMEM
    return pl.pallas_call(
        kernel,
        out_shape=(
            jax.ShapeDtypeStruct((faces, nsel, width), jnp.float32),
            jax.ShapeDtypeStruct((faces, nsel, nsel), jnp.float32),
        ),
        in_specs=[pl.BlockSpec(memory_space=smem)] * len(smem_args)
        + [pl.BlockSpec(memory_space=vmem)] * len(vmem_args),
        out_specs=(pl.BlockSpec(memory_space=vmem), pl.BlockSpec(memory_space=vmem)),
        scratch_shapes=[
            pltpu.VMEM((faces, width, width), jnp.float32),
            pltpu.VMEM((faces, count, width), jnp.float32),
            pltpu.VMEM((faces, count, width), jnp.float32),
            pltpu.VMEM((faces, count, count), jnp.float32),
        ],
        compiler_params=pltpu.CompilerParams(vmem_limit_bytes=60 * 1024 * 1024),
    )(*smem_args, *vmem_args)


def per_device(
    plus_blocks, minus_blocks, inner_blocks, initial_subspace, picks, owner, material_class, coef
):
    plus_local = plus_blocks[0, 0, 0]
    minus_local = minus_blocks[0, 0, 0]
    inner_local = inner_blocks[0, 0, 0]
    basis_vectors = initial_subspace[0, 0, 0]
    picks_flat = picks[0, 0, 0].reshape(-1)
    dims, crossing, width = plus_local.shape[0], plus_local.shape[1], plus_local.shape[-1]
    faces_all, count = basis_vectors.shape[0], basis_vectors.shape[1]
    nsel = picks.shape[-1]
    pairs = crossing // 2
    matches = material_class.reshape(()) == jnp.arange(coef.shape[0], dtype=jnp.int32)
    own_scale = jnp.sum(jnp.where(matches, coef, 0.0))
    row = lax.broadcasted_iota(jnp.int32, (width, width), 0)
    col = lax.broadcasted_iota(jnp.int32, (width, width), 1)
    axes = ("gx", "gy", "gz")
    packed_in = []
    side_in = []
    for a in range(dims):
        halves = minus_local[a]
        packed = jnp.where(col >= row, halves[:pairs], halves[pairs:])
        diagonals = jnp.sum(jnp.where(col == row, halves[pairs:], 0.0), axis=1)
        side = jnp.concatenate([diagonals, jnp.broadcast_to(own_scale, (1, width))], axis=0)
        packed_in.append(passed_along(packed, axes[a], -1))
        side_in.append(passed_along(side, axes[a], -1))

    scal = own_scale.reshape(1)
    n_inner = inner_local.shape[1]
    inner_c, inner_e = run_faces(
        inner_kernel, n_inner, nsel, width, count, (scal, picks_flat), (inner_local, basis_vectors)
    )
    cross_c, cross_e = run_faces(
        cross_kernel, dims * crossing, nsel, width, count, (scal, picks_flat),
        (plus_local, *packed_in, *side_in, basis_vectors),
    )
    constraints = jnp.concatenate([cross_c, inner_c], axis=0)
    blocks = jnp.concatenate([cross_e, inner_e], axis=0)
    flat = blocks.reshape(faces_all, -1)
    groups = lax.axis_size("gz")
    rows_all = groups * CROWS
    owner_hot = (owner[0, 0, 0][:, None] == jnp.arange(rows_all, dtype=jnp.int32)).astype(jnp.float32)
    term = jnp.einsum("fr,fe->re", owner_hot, flat, precision=HIGHEST).reshape(groups, CROWS, -1)
    me = lax.axis_index("gz")
    coarse = lax.dynamic_index_in_dim(term, me, 0, keepdims=False)
    for shift in range(1, groups):
        part = lax.dynamic_index_in_dim(term, (me + shift) % groups, 0, keepdims=False)
        route = [(i, (i + shift) % groups) for i in range(groups)]
        coarse = coarse + lax.ppermute(part, "gz", route)
    return (constraints[None, None, None], coarse[None, None])


def solution(mesh):
    return jax.shard_map(
        per_device,
        mesh=mesh,
        in_specs=(
            P("gx", "gy", "gz", None, None, None, None),
            P("gx", "gy", "gz", None, None, None, None),
            P("gx", "gy", "gz", None, None, None, None),
            P("gx", "gy", "gz", None, None, None),
            P("gx", "gy", "gz", None, None),
            P("gx", "gy", "gz", None),
            P("gx", "gy", "gz"),
            P(),
        ),
        out_specs=(P("gx", "gy", "gz", None, None, None), P("gx", "gy", "gz", None)),
        check_vma=False,
    )
```

```python
import math

import jax
import jax.numpy as jnp
from jax import lax
from jax.experimental import pallas as pl
from jax.experimental.pallas import tpu as pltpu
from jax.sharding import PartitionSpec as P

ITERS = 4
CROWS = 16
HIGHEST = lax.Precision.HIGHEST


def passed_along(block, axis, distance):
    devices = range(lax.axis_size(axis))
    route = [(i - distance, i) for i in devices if i - distance in devices]
    return lax.ppermute(block, axis, route)


GROUP = 8


def eliminate(grams, count):
    state = []
    for gram in grams:
        faces = gram.shape[0] // count
        shape = (faces, count, gram.shape[1])
        face = lax.broadcasted_iota(jnp.int32, shape, 0)
        sub = lax.broadcasted_iota(jnp.int32, shape, 1)
        lane = lax.broadcasted_iota(jnp.int32, shape, 2)
        base = face * count
        left = jnp.where(lane // count == face, gram.reshape(shape), 0.0)
        right = (lane == base + sub).astype(jnp.float32)
        state.append([left, right, sub, lane, base])
    for j in range(count):
        for item in state:
            left, right, sub, lane, base = item
            row_l = jnp.sum(jnp.where(sub == j, left, 0.0), axis=1, keepdims=True)
            row_r = jnp.sum(jnp.where(sub == j, right, 0.0), axis=1, keepdims=True)
            at_pivot = lane == base + j
            pivot = jnp.sum(jnp.where(at_pivot[:, :1], row_l, 0.0), axis=2, keepdims=True)
            inv = 1.0 / jnp.sqrt(pivot)
            col = jnp.sum(jnp.where(at_pivot, left, 0.0), axis=2, keepdims=True) * inv
            col = jnp.where(sub[:, :, :1] > j, col, 0.0)
            row_l = row_l * inv
            row_r = row_r * inv
            item[0] = jnp.where(sub == j, row_l, left - col * row_l)
            item[1] = jnp.where(sub == j, row_r, right - col * row_r)
    return [item[1].reshape(item[1].shape[0] * count, -1) for item in state]


def iterate(own, picks_ref, pick_base, c_ref, e_ref, m_scr, v_scr, w_scr):
    faces, count = v_scr.shape[0], v_scr.shape[1]
    nsel = c_ref.shape[1]
    scale_out = math.sqrt(m_scr.shape[-1])
    spans = [(g, min(g + GROUP, faces)) for g in range(0, faces, GROUP)]

    def image(f, carry):
        w_scr[f] = jnp.dot(v_scr[f], m_scr[f], precision=HIGHEST, preferred_element_type=jnp.float32)
        return carry

    for iteration in range(ITERS):
        lax.fori_loop(0, faces, image, 0, unroll=4)
        images = [w_scr[g0:g1].reshape((g1 - g0) * count, -1) for g0, g1 in spans]
        grams = [
            lax.dot_general(
                w, w, (((1,), (1,)), ((), ())), precision=HIGHEST, preferred_element_type=jnp.float32
            )
            for w in images
        ]
        inverses = eliminate(grams, count)
        for (g0, g1), inverse, w in zip(spans, inverses, images):
            solved = jnp.dot(inverse, w, precision=HIGHEST, preferred_element_type=jnp.float32)
            v_scr[g0:g1] = solved.reshape(g1 - g0, count, -1)

    def finish(f, carry):
        rows = [v_scr[f, pl.ds(picks_ref[pick_base + f * nsel + s], 1), :] for s in range(nsel)]
        picked = jnp.concatenate(rows, axis=0)
        c_ref[f] = picked * scale_out
        images = jnp.dot(picked, m_scr[f], precision=HIGHEST, preferred_element_type=jnp.float32)
        block = lax.dot_general(
            picked, images, (((1,), (1,)), ((), ())), precision=HIGHEST, preferred_element_type=jnp.float32
        )
        e_ref[f] = block / own
        return carry

    lax.fori_loop(0, faces, finish, 0, unroll=2)


def inner_kernel(scal_ref, picks_ref, inner_ref, v0_ref, c_ref, e_ref, m_scr, v_scr, w_scr):
    faces = m_scr.shape[0]
    base = v0_ref.shape[0] - faces
    own = scal_ref[0]
    for f in range(faces):
        m_scr[f] = own * inner_ref[0, f] + own * inner_ref[1, f]
        v_scr[f] = v0_ref[base + f]
    iterate(own, picks_ref, base * c_ref.shape[1], c_ref, e_ref, m_scr, v_scr, w_scr)


def unpacked(packed, side, index, pairs):
    width = packed.shape[-1]
    row = lax.broadcasted_iota(jnp.int32, (width, width), 0)
    col = lax.broadcasted_iota(jnp.int32, (width, width), 1)
    start = (index % pairs) * width
    mixed = packed[start : start + width, :]
    turned = mixed.T
    if index < pairs:
        return jnp.where(col >= row, mixed, turned)
    diagonal = side[index - pairs : index - pairs + 1, :]
    return jnp.where(col > row, turned, jnp.where(col == row, diagonal, mixed))


def cross_kernel(scal_ref, picks_ref, plus_ref, *refs):
    dims = plus_ref.shape[0]
    packed_refs = refs[:dims]
    v0_ref, c_ref, e_ref, m_scr, v_scr, w_scr = refs[dims:]
    crossing, width = plus_ref.shape[1], plus_ref.shape[-1]
    pairs = crossing // 2
    own = scal_ref[0]
    for a in range(dims):
        packed = packed_refs[a]
        side = packed[pairs * width :, :]
        next_scale = side[pairs : pairs + 1, 0:1]
        for k in range(crossing):
            f = a * crossing + k
            m_scr[f] = own * plus_ref[a, k] + next_scale * unpacked(packed, side, k, pairs)
            v_scr[f] = v0_ref[f]
    iterate(own, picks_ref, 0, c_ref, e_ref, m_scr, v_scr, w_scr)


def run_faces(kernel, faces, nsel, width, count, smem_args, vmem_args):
    vmem = pltpu.MemorySpace.VMEM
    smem = pltpu.MemorySpace.SMEM
    return pl.pallas_call(
        kernel,
        out_shape=(
            jax.ShapeDtypeStruct((faces, nsel, width), jnp.float32),
            jax.ShapeDtypeStruct((faces, nsel, nsel), jnp.float32),
        ),
        in_specs=[pl.BlockSpec(memory_space=smem)] * len(smem_args)
        + [pl.BlockSpec(memory_space=vmem)] * len(vmem_args),
        out_specs=(pl.BlockSpec(memory_space=vmem), pl.BlockSpec(memory_space=vmem)),
        scratch_shapes=[
            pltpu.VMEM((faces, width, width), jnp.float32),
            pltpu.VMEM((faces, count, width), jnp.float32),
            pltpu.VMEM((faces, count, width), jnp.float32),
        ],
        compiler_params=pltpu.CompilerParams(vmem_limit_bytes=60 * 1024 * 1024),
    )(*smem_args, *vmem_args)


def per_device(
    plus_blocks, minus_blocks, inner_blocks, initial_subspace, picks, owner, material_class, coef
):
    plus_local = plus_blocks[0, 0, 0]
    minus_local = minus_blocks[0, 0, 0]
    inner_local = inner_blocks[0, 0, 0]
    basis_vectors = initial_subspace[0, 0, 0]
    picks_flat = picks[0, 0, 0].reshape(-1)
    dims, crossing, width = plus_local.shape[0], plus_local.shape[1], plus_local.shape[-1]
    faces_all, count = basis_vectors.shape[0], basis_vectors.shape[1]
    nsel = picks.shape[-1]
    pairs = crossing // 2
    matches = material_class.reshape(()) == jnp.arange(coef.shape[0], dtype=jnp.int32)
    own_scale = jnp.sum(jnp.where(matches, coef, 0.0))
    row = lax.broadcasted_iota(jnp.int32, (width, width), 0)
    col = lax.broadcasted_iota(jnp.int32, (width, width), 1)
    axes = ("gx", "gy", "gz")
    packed_in = []
    for a in range(dims):
        halves = minus_local[a]
        packed = jnp.where(col >= row, halves[:pairs], halves[pairs:]).reshape(pairs * width, width)
        diagonals = jnp.sum(jnp.where(col == row, halves[pairs:], 0.0), axis=1)
        scale_row = jnp.broadcast_to(own_scale, (1, width))
        pad = jnp.zeros((-(pairs + 1) % 8, width), jnp.float32)
        message = jnp.concatenate([packed, diagonals, scale_row, pad], axis=0)
        packed_in.append(passed_along(message, axes[a], -1))

    scal = own_scale.reshape(1)
    n_inner = inner_local.shape[1]
    inner_c, inner_e = run_faces(
        inner_kernel, n_inner, nsel, width, count, (scal, picks_flat), (inner_local, basis_vectors)
    )
    cross_c, cross_e = run_faces(
        cross_kernel, dims * crossing, nsel, width, count, (scal, picks_flat),
        (plus_local, *packed_in, basis_vectors),
    )
    constraints = jnp.concatenate([cross_c, inner_c], axis=0)
    blocks = jnp.concatenate([cross_e, inner_e], axis=0)
    flat = blocks.reshape(faces_all, -1)
    groups = lax.axis_size("gz")
    rows_all = groups * CROWS
    owner_hot = (owner[0, 0, 0][:, None] == jnp.arange(rows_all, dtype=jnp.int32)).astype(jnp.float32)
    term = jnp.einsum("fr,fe->re", owner_hot, flat, precision=HIGHEST).reshape(groups, CROWS, -1)
    me = lax.axis_index("gz")
    coarse = lax.dynamic_index_in_dim(term, me, 0, keepdims=False)
    for shift in range(1, groups):
        part = lax.dynamic_index_in_dim(term, (me + shift) % groups, 0, keepdims=False)
        route = [(i, (i + shift) % groups) for i in range(groups)]
        coarse = coarse + lax.ppermute(part, "gz", route)
    return (constraints[None, None, None], coarse[None, None])


def solution(mesh):
    return jax.shard_map(
        per_device,
        mesh=mesh,
        in_specs=(
            P("gx", "gy", "gz", None, None, None, None),
            P("gx", "gy", "gz", None, None, None, None),
            P("gx", "gy", "gz", None, None, None, None),
            P("gx", "gy", "gz", None, None, None),
            P("gx", "gy", "gz", None, None),
            P("gx", "gy", "gz", None),
            P("gx", "gy", "gz"),
            P(),
        ),
        out_specs=(P("gx", "gy", "gz", None, None, None), P("gx", "gy", "gz", None)),
        check_vma=False,
    )
```

```python
import functools
import math

import jax
import jax.numpy as jnp
from jax import lax
from jax.experimental import pallas as pl
from jax.experimental.pallas import tpu as pltpu
from jax.sharding import PartitionSpec as P

ITERS = 4
CROWS = 16
HIGHEST = lax.Precision.HIGHEST


def passed_along(block, axis, distance):
    devices = range(lax.axis_size(axis))
    route = [(i - distance, i) for i in devices if i - distance in devices]
    return lax.ppermute(block, axis, route)


GROUP = 8


def eliminate(grams, count):
    state = []
    for gram in grams:
        faces = gram.shape[0] // count
        shape = (faces, count, gram.shape[1])
        face = lax.broadcasted_iota(jnp.int32, shape, 0)
        sub = lax.broadcasted_iota(jnp.int32, shape, 1)
        lane = lax.broadcasted_iota(jnp.int32, shape, 2)
        base = face * count
        left = jnp.where(lane // count == face, gram.reshape(shape), 0.0)
        right = (lane == base + sub).astype(jnp.float32)
        state.append([left, right, sub, lane, base])
    for j in range(count):
        for item in state:
            left, right, sub, lane, base = item
            row_l = jnp.sum(jnp.where(sub == j, left, 0.0), axis=1, keepdims=True)
            row_r = jnp.sum(jnp.where(sub == j, right, 0.0), axis=1, keepdims=True)
            at_pivot = lane == base + j
            pivot = jnp.sum(jnp.where(at_pivot[:, :1], row_l, 0.0), axis=2, keepdims=True)
            inv = 1.0 / jnp.sqrt(pivot)
            col = jnp.sum(jnp.where(at_pivot, left, 0.0), axis=2, keepdims=True) * inv
            col = jnp.where(sub[:, :, :1] > j, col, 0.0)
            row_l = row_l * inv
            row_r = row_r * inv
            item[0] = jnp.where(sub == j, row_l, left - col * row_l)
            item[1] = jnp.where(sub == j, row_r, right - col * row_r)
    return [item[1].reshape(item[1].shape[0] * count, -1) for item in state]


def iterate(own, picks_ref, first, c_ref, e_ref, m_scr, v_scr, w_scr):
    faces, count = v_scr.shape[0], v_scr.shape[1]
    nsel = c_ref.shape[1]
    scale_out = math.sqrt(m_scr.shape[-1])
    spans = [(g, min(g + GROUP, faces)) for g in range(0, faces, GROUP)]

    def image(f, carry):
        w_scr[f] = jnp.dot(v_scr[f], m_scr[f], precision=HIGHEST, preferred_element_type=jnp.float32)
        return carry

    for iteration in range(ITERS):
        lax.fori_loop(0, faces, image, 0, unroll=4)
        images = [w_scr[g0:g1].reshape((g1 - g0) * count, -1) for g0, g1 in spans]
        grams = [
            lax.dot_general(
                w, w, (((1,), (1,)), ((), ())), precision=HIGHEST, preferred_element_type=jnp.float32
            )
            for w in images
        ]
        inverses = eliminate(grams, count)
        for (g0, g1), inverse, w in zip(spans, inverses, images):
            solved = jnp.dot(inverse, w, precision=HIGHEST, preferred_element_type=jnp.float32)
            v_scr[g0:g1] = solved.reshape(g1 - g0, count, -1)

    def finish(f, carry):
        rows = [v_scr[f, pl.ds(picks_ref[(first + f) * nsel + s], 1), :] for s in range(nsel)]
        picked = jnp.concatenate(rows, axis=0)
        c_ref[first + f] = picked * scale_out
        images = jnp.dot(picked, m_scr[f], precision=HIGHEST, preferred_element_type=jnp.float32)
        block = lax.dot_general(
            picked, images, (((1,), (1,)), ((), ())), precision=HIGHEST, preferred_element_type=jnp.float32
        )
        e_ref[first + f] = block / own
        return carry

    lax.fori_loop(0, faces, finish, 0, unroll=2)


def unpacked(packed, side, index, pairs):
    width = packed.shape[-1]
    row = lax.broadcasted_iota(jnp.int32, (width, width), 0)
    col = lax.broadcasted_iota(jnp.int32, (width, width), 1)
    start = (index % pairs) * width
    mixed = packed[start : start + width, :]
    turned = mixed.T
    if index < pairs:
        return jnp.where(col >= row, mixed, turned)
    diagonal = side[index - pairs : index - pairs + 1, :]
    return jnp.where(col > row, turned, jnp.where(col == row, diagonal, mixed))


def face_kernel(cross_axes, with_inner, scal_ref, picks_ref, plus_ref, *refs):
    packed_refs = refs[: len(cross_axes)]
    rest = refs[len(cross_axes) :]
    inner_ref = rest[0] if with_inner else None
    rest = rest[1:] if with_inner else rest
    v0_ref = rest[0]
    c_ref, e_ref, m_scr, v_scr, w_scr = rest[-5:]
    if len(rest) > 6:
        c_ref[...] = rest[1][...]
        e_ref[...] = rest[2][...]
    crossing, width = plus_ref.shape[1], plus_ref.shape[-1]
    pairs = crossing // 2
    first = cross_axes[0] * crossing
    own = scal_ref[0]
    f = 0
    for a, packed in zip(cross_axes, packed_refs):
        side = packed[pairs * width :, :]
        next_scale = side[pairs : pairs + 1, 0:1]
        for k in range(crossing):
            m_scr[f] = own * plus_ref[a, k] + next_scale * unpacked(packed, side, k, pairs)
            v_scr[f] = v0_ref[first + f]
            f += 1
    if with_inner:
        for k in range(inner_ref.shape[1]):
            m_scr[f] = own * inner_ref[0, k] + own * inner_ref[1, k]
            v_scr[f] = v0_ref[first + f]
            f += 1
    iterate(own, picks_ref, first, c_ref, e_ref, m_scr, v_scr, w_scr)


def run_faces(kernel, faces, nsel, width, count, smem_args, vmem_args, earlier=()):
    vmem = pltpu.MemorySpace.VMEM
    smem = pltpu.MemorySpace.SMEM
    total = vmem_args[-1].shape[0]
    args = (*smem_args, *vmem_args, *earlier)
    aliases = {len(args) - len(earlier) + i: i for i in range(len(earlier))}
    return pl.pallas_call(
        kernel,
        out_shape=(
            jax.ShapeDtypeStruct((total, nsel, width), jnp.float32),
            jax.ShapeDtypeStruct((total, nsel, nsel), jnp.float32),
        ),
        in_specs=[pl.BlockSpec(memory_space=smem)] * len(smem_args)
        + [pl.BlockSpec(memory_space=vmem)] * (len(vmem_args) + len(earlier)),
        out_specs=(pl.BlockSpec(memory_space=vmem), pl.BlockSpec(memory_space=vmem)),
        scratch_shapes=[
            pltpu.VMEM((faces, width, width), jnp.float32),
            pltpu.VMEM((faces, count, width), jnp.float32),
            pltpu.VMEM((faces, count, width), jnp.float32),
        ],
        input_output_aliases=aliases,
        compiler_params=pltpu.CompilerParams(vmem_limit_bytes=60 * 1024 * 1024),
    )(*args)


def per_device(
    plus_blocks, minus_blocks, inner_blocks, initial_subspace, picks, owner, material_class, coef
):
    plus_local = plus_blocks[0, 0, 0]
    minus_local = minus_blocks[0, 0, 0]
    inner_local = inner_blocks[0, 0, 0]
    basis_vectors = initial_subspace[0, 0, 0]
    picks_flat = picks[0, 0, 0].reshape(-1)
    dims, crossing, width = plus_local.shape[0], plus_local.shape[1], plus_local.shape[-1]
    faces_all, count = basis_vectors.shape[0], basis_vectors.shape[1]
    nsel = picks.shape[-1]
    pairs = crossing // 2
    matches = material_class.reshape(()) == jnp.arange(coef.shape[0], dtype=jnp.int32)
    own_scale = jnp.sum(jnp.where(matches, coef, 0.0))
    row = lax.broadcasted_iota(jnp.int32, (width, width), 0)
    col = lax.broadcasted_iota(jnp.int32, (width, width), 1)
    axes = ("gx", "gy", "gz")
    packed_in = []
    for a in range(dims):
        halves = minus_local[a]
        packed = jnp.where(col >= row, halves[:pairs], halves[pairs:]).reshape(pairs * width, width)
        diagonals = jnp.sum(jnp.where(col == row, halves[pairs:], 0.0), axis=1)
        scale_row = jnp.broadcast_to(own_scale, (1, width))
        pad = jnp.zeros((-(pairs + 1) % 8, width), jnp.float32)
        message = jnp.concatenate([packed, diagonals, scale_row, pad], axis=0)
        packed_in.append(passed_along(message, axes[a], -1))

    scal = own_scale.reshape(1)
    n_inner = inner_local.shape[1]
    late = tuple(range(dims - 1))
    early_c, early_e = run_faces(
        functools.partial(face_kernel, (dims - 1,), True), crossing + n_inner, nsel, width, count,
        (scal, picks_flat), (plus_local, packed_in[dims - 1], inner_local, basis_vectors),
    )
    constraints, blocks = run_faces(
        functools.partial(face_kernel, late, False), len(late) * crossing, nsel, width, count,
        (scal, picks_flat), (plus_local, *packed_in[: dims - 1], basis_vectors), (early_c, early_e),
    )
    flat = blocks.reshape(faces_all, -1)
    groups = lax.axis_size("gz")
    rows_all = groups * CROWS
    owner_hot = (owner[0, 0, 0][:, None] == jnp.arange(rows_all, dtype=jnp.int32)).astype(jnp.float32)
    term = jnp.einsum("fr,fe->re", owner_hot, flat, precision=HIGHEST).reshape(groups, CROWS, -1)
    coarse = jnp.sum(lax.all_to_all(term, "gz", 0, 0), axis=0)
    return (constraints[None, None, None], coarse[None, None])


def solution(mesh):
    return jax.shard_map(
        per_device,
        mesh=mesh,
        in_specs=(
            P("gx", "gy", "gz", None, None, None, None),
            P("gx", "gy", "gz", None, None, None, None),
            P("gx", "gy", "gz", None, None, None, None),
            P("gx", "gy", "gz", None, None, None),
            P("gx", "gy", "gz", None, None),
            P("gx", "gy", "gz", None),
            P("gx", "gy", "gz"),
            P(),
        ),
        out_specs=(P("gx", "gy", "gz", None, None, None), P("gx", "gy", "gz", None)),
        check_vma=False,
    )
```

```python
import functools
import math

import jax
import jax.numpy as jnp
from jax import lax
from jax.experimental import pallas as pl
from jax.experimental.pallas import tpu as pltpu
from jax.sharding import PartitionSpec as P

ITERS = 4
CROWS = 16
HIGHEST = lax.Precision.HIGHEST


def passed_along(block, axis, distance):
    devices = range(lax.axis_size(axis))
    route = [(i - distance, i) for i in devices if i - distance in devices]
    return lax.ppermute(block, axis, route)


GROUP = 8


def eliminate(grams, count):
    state = []
    for gram in grams:
        faces = gram.shape[0] // count
        shape = (faces, count, gram.shape[1])
        face = lax.broadcasted_iota(jnp.int32, shape, 0)
        sub = lax.broadcasted_iota(jnp.int32, shape, 1)
        lane = lax.broadcasted_iota(jnp.int32, shape, 2)
        base = face * count
        left = jnp.where(lane // count == face, gram.reshape(shape), 0.0)
        right = (lane == base + sub).astype(jnp.float32)
        state.append([left, right, sub, lane, base])
    for j in range(count):
        for item in state:
            left, right, sub, lane, base = item
            row_l = jnp.sum(jnp.where(sub == j, left, 0.0), axis=1, keepdims=True)
            row_r = jnp.sum(jnp.where(sub == j, right, 0.0), axis=1, keepdims=True)
            at_pivot = lane == base + j
            pivot = jnp.sum(jnp.where(at_pivot[:, :1], row_l, 0.0), axis=2, keepdims=True)
            inv = 1.0 / jnp.sqrt(pivot)
            col = jnp.sum(jnp.where(at_pivot, left, 0.0), axis=2, keepdims=True) * inv
            col = jnp.where(sub[:, :, :1] > j, col, 0.0)
            row_l = row_l * inv
            row_r = row_r * inv
            item[0] = jnp.where(sub == j, row_l, left - col * row_l)
            item[1] = jnp.where(sub == j, row_r, right - col * row_r)
    return [item[1].reshape(item[1].shape[0] * count, -1) for item in state]


def iterate(own, picks_ref, first, c_ref, e_ref, m_scr, v_scr, w_scr):
    faces, count = v_scr.shape[0], v_scr.shape[1]
    nsel = c_ref.shape[1]
    scale_out = math.sqrt(m_scr.shape[-1])
    spans = [(g, min(g + GROUP, faces)) for g in range(0, faces, GROUP)]

    def image(f, carry):
        w_scr[f] = jnp.dot(v_scr[f], m_scr[f], precision=lax.Precision.HIGH, preferred_element_type=jnp.float32)
        return carry

    for iteration in range(ITERS):
        lax.fori_loop(0, faces, image, 0, unroll=4)
        images = [w_scr[g0:g1].reshape((g1 - g0) * count, -1) for g0, g1 in spans]
        grams = [
            lax.dot_general(
                w, w, (((1,), (1,)), ((), ())), precision=HIGHEST, preferred_element_type=jnp.float32
            )
            for w in images
        ]
        inverses = eliminate(grams, count)
        for (g0, g1), inverse, w in zip(spans, inverses, images):
            solved = jnp.dot(inverse, w, precision=HIGHEST, preferred_element_type=jnp.float32)
            v_scr[g0:g1] = solved.reshape(g1 - g0, count, -1)

    def finish(f, carry):
        rows = [v_scr[f, pl.ds(picks_ref[(first + f) * nsel + s], 1), :] for s in range(nsel)]
        picked = jnp.concatenate(rows, axis=0)
        c_ref[first + f] = picked * scale_out
        images = jnp.dot(picked, m_scr[f], precision=HIGHEST, preferred_element_type=jnp.float32)
        block = lax.dot_general(
            picked, images, (((1,), (1,)), ((), ())), precision=HIGHEST, preferred_element_type=jnp.float32
        )
        e_ref[first + f] = block / own
        return carry

    lax.fori_loop(0, faces, finish, 0, unroll=2)


def unpacked(packed, side, index, pairs):
    width = packed.shape[-1]
    row = lax.broadcasted_iota(jnp.int32, (width, width), 0)
    col = lax.broadcasted_iota(jnp.int32, (width, width), 1)
    start = (index % pairs) * width
    mixed = packed[start : start + width, :]
    turned = mixed.T
    if index < pairs:
        return jnp.where(col >= row, mixed, turned)
    diagonal = side[index - pairs : index - pairs + 1, :]
    return jnp.where(col > row, turned, jnp.where(col == row, diagonal, mixed))


def face_kernel(cross_axes, with_inner, scal_ref, picks_ref, plus_ref, *refs):
    packed_refs = refs[: len(cross_axes)]
    rest = refs[len(cross_axes) :]
    inner_ref = rest[0] if with_inner else None
    rest = rest[1:] if with_inner else rest
    v0_ref = rest[0]
    c_ref, e_ref, m_scr, v_scr, w_scr = rest[-5:]
    if len(rest) > 6:
        c_ref[...] = rest[1][...]
        e_ref[...] = rest[2][...]
    crossing, width = plus_ref.shape[1], plus_ref.shape[-1]
    pairs = crossing // 2
    first = cross_axes[0] * crossing
    own = scal_ref[0]
    f = 0
    for a, packed in zip(cross_axes, packed_refs):
        side = packed[pairs * width :, :]
        next_scale = side[pairs : pairs + 1, 0:1]
        for k in range(crossing):
            m_scr[f] = own * plus_ref[a, k] + next_scale * unpacked(packed, side, k, pairs)
            v_scr[f] = v0_ref[first + f]
            f += 1
    if with_inner:
        for k in range(inner_ref.shape[1]):
            m_scr[f] = own * inner_ref[0, k] + own * inner_ref[1, k]
            v_scr[f] = v0_ref[first + f]
            f += 1
    iterate(own, picks_ref, first, c_ref, e_ref, m_scr, v_scr, w_scr)


def run_faces(kernel, faces, nsel, width, count, smem_args, vmem_args, earlier=()):
    vmem = pltpu.MemorySpace.VMEM
    smem = pltpu.MemorySpace.SMEM
    total = vmem_args[-1].shape[0]
    args = (*smem_args, *vmem_args, *earlier)
    aliases = {len(args) - len(earlier) + i: i for i in range(len(earlier))}
    return pl.pallas_call(
        kernel,
        out_shape=(
            jax.ShapeDtypeStruct((total, nsel, width), jnp.float32),
            jax.ShapeDtypeStruct((total, nsel, nsel), jnp.float32),
        ),
        in_specs=[pl.BlockSpec(memory_space=smem)] * len(smem_args)
        + [pl.BlockSpec(memory_space=vmem)] * (len(vmem_args) + len(earlier)),
        out_specs=(pl.BlockSpec(memory_space=vmem), pl.BlockSpec(memory_space=vmem)),
        scratch_shapes=[
            pltpu.VMEM((faces, width, width), jnp.float32),
            pltpu.VMEM((faces, count, width), jnp.float32),
            pltpu.VMEM((faces, count, width), jnp.float32),
        ],
        input_output_aliases=aliases,
        compiler_params=pltpu.CompilerParams(vmem_limit_bytes=60 * 1024 * 1024),
    )(*args)


def per_device(
    plus_blocks, minus_blocks, inner_blocks, initial_subspace, picks, owner, material_class, coef
):
    plus_local = plus_blocks[0, 0, 0]
    minus_local = minus_blocks[0, 0, 0]
    inner_local = inner_blocks[0, 0, 0]
    basis_vectors = initial_subspace[0, 0, 0]
    picks_flat = picks[0, 0, 0].reshape(-1)
    dims, crossing, width = plus_local.shape[0], plus_local.shape[1], plus_local.shape[-1]
    faces_all, count = basis_vectors.shape[0], basis_vectors.shape[1]
    nsel = picks.shape[-1]
    pairs = crossing // 2
    matches = material_class.reshape(()) == jnp.arange(coef.shape[0], dtype=jnp.int32)
    own_scale = jnp.sum(jnp.where(matches, coef, 0.0))
    row = lax.broadcasted_iota(jnp.int32, (width, width), 0)
    col = lax.broadcasted_iota(jnp.int32, (width, width), 1)
    axes = ("gx", "gy", "gz")
    packed_in = []
    for a in range(dims):
        halves = minus_local[a]
        packed = jnp.where(col >= row, halves[:pairs], halves[pairs:]).reshape(pairs * width, width)
        diagonals = jnp.sum(jnp.where(col == row, halves[pairs:], 0.0), axis=1)
        scale_row = jnp.broadcast_to(own_scale, (1, width))
        pad = jnp.zeros((-(pairs + 1) % 8, width), jnp.float32)
        message = jnp.concatenate([packed, diagonals, scale_row, pad], axis=0)
        packed_in.append(passed_along(message, axes[a], -1))

    scal = own_scale.reshape(1)
    n_inner = inner_local.shape[1]
    late = tuple(range(dims - 1))
    early_c, early_e = run_faces(
        functools.partial(face_kernel, (dims - 1,), True), crossing + n_inner, nsel, width, count,
        (scal, picks_flat), (plus_local, packed_in[dims - 1], inner_local, basis_vectors),
    )
    constraints, blocks = run_faces(
        functools.partial(face_kernel, late, False), len(late) * crossing, nsel, width, count,
        (scal, picks_flat), (plus_local, *packed_in[: dims - 1], basis_vectors), (early_c, early_e),
    )
    flat = blocks.reshape(faces_all, -1)
    groups = lax.axis_size("gz")
    rows_all = groups * CROWS
    owner_hot = (owner[0, 0, 0][:, None] == jnp.arange(rows_all, dtype=jnp.int32)).astype(jnp.float32)
    term = jnp.einsum("fr,fe->re", owner_hot, flat, precision=HIGHEST).reshape(groups, CROWS, -1)
    coarse = jnp.sum(lax.all_to_all(term, "gz", 0, 0), axis=0)
    return (constraints[None, None, None], coarse[None, None])


def solution(mesh):
    return jax.shard_map(
        per_device,
        mesh=mesh,
        in_specs=(
            P("gx", "gy", "gz", None, None, None, None),
            P("gx", "gy", "gz", None, None, None, None),
            P("gx", "gy", "gz", None, None, None, None),
            P("gx", "gy", "gz", None, None, None),
            P("gx", "gy", "gz", None, None),
            P("gx", "gy", "gz", None),
            P("gx", "gy", "gz"),
            P(),
        ),
        out_specs=(P("gx", "gy", "gz", None, None, None), P("gx", "gy", "gz", None)),
        check_vma=False,
    )
```

```python
import functools
import math

import jax
import jax.numpy as jnp
from jax import lax
from jax.experimental import pallas as pl
from jax.experimental.pallas import tpu as pltpu
from jax.sharding import PartitionSpec as P

ITERS = 4
CROWS = 16
HIGHEST = lax.Precision.HIGHEST


def passed_along(block, axis, distance):
    devices = range(lax.axis_size(axis))
    route = [(i - distance, i) for i in devices if i - distance in devices]
    return lax.ppermute(block, axis, route)


GROUP = 8


def eliminate(grams, count):
    state = []
    for gram in grams:
        faces = gram.shape[0] // count
        shape = (faces, count, gram.shape[1])
        face = lax.broadcasted_iota(jnp.int32, shape, 0)
        sub = lax.broadcasted_iota(jnp.int32, shape, 1)
        lane = lax.broadcasted_iota(jnp.int32, shape, 2)
        base = face * count
        left = jnp.where(lane // count == face, gram.reshape(shape), 0.0)
        right = (lane == base + sub).astype(jnp.float32)
        state.append([left, right, sub, lane, base])
    for j in range(count):
        for item in state:
            left, right, sub, lane, base = item
            row_l = jnp.sum(jnp.where(sub == j, left, 0.0), axis=1, keepdims=True)
            row_r = jnp.sum(jnp.where(sub == j, right, 0.0), axis=1, keepdims=True)
            at_pivot = lane == base + j
            pivot = jnp.sum(jnp.where(at_pivot[:, :1], row_l, 0.0), axis=2, keepdims=True)
            inv = 1.0 / jnp.sqrt(pivot)
            col = jnp.sum(jnp.where(at_pivot, left, 0.0), axis=2, keepdims=True) * inv
            col = jnp.where(sub[:, :, :1] > j, col, 0.0)
            row_l = row_l * inv
            row_r = row_r * inv
            item[0] = jnp.where(sub == j, row_l, left - col * row_l)
            item[1] = jnp.where(sub == j, row_r, right - col * row_r)
    return [item[1].reshape(item[1].shape[0] * count, -1) for item in state]


def iterate(own, picks_ref, first, c_ref, e_ref, m_scr, v_scr, w_scr):
    faces, count = v_scr.shape[0], v_scr.shape[1]
    nsel = c_ref.shape[1]
    scale_out = math.sqrt(m_scr.shape[-1])
    spans = [(g, min(g + GROUP, faces)) for g in range(0, faces, GROUP)]

    def image(f, carry):
        w_scr[f] = jnp.dot(v_scr[f], m_scr[f], precision=HIGHEST, preferred_element_type=jnp.float32)
        return carry

    for iteration in range(ITERS):
        lax.fori_loop(0, faces, image, 0, unroll=4)
        images = [w_scr[g0:g1].reshape((g1 - g0) * count, -1) for g0, g1 in spans]
        grams = [
            lax.dot_general(
                w, w, (((1,), (1,)), ((), ())), precision=HIGHEST, preferred_element_type=jnp.float32
            )
            for w in images
        ]
        inverses = eliminate(grams, count)
        for (g0, g1), inverse, w in zip(spans, inverses, images):
            solved = jnp.dot(inverse, w, precision=HIGHEST, preferred_element_type=jnp.float32)
            v_scr[g0:g1] = solved.reshape(g1 - g0, count, -1)

    def finish(f, carry):
        rows = [v_scr[f, pl.ds(picks_ref[(first + f) * nsel + s], 1), :] for s in range(nsel)]
        picked = jnp.concatenate(rows, axis=0)
        c_ref[first + f] = picked * scale_out
        images = jnp.dot(picked, m_scr[f], precision=HIGHEST, preferred_element_type=jnp.float32)
        block = lax.dot_general(
            picked, images, (((1,), (1,)), ((), ())), precision=HIGHEST, preferred_element_type=jnp.float32
        )
        e_ref[first + f] = block / own
        return carry

    lax.fori_loop(0, faces, finish, 0, unroll=2)


def unpacked(packed, side, index, pairs):
    width = packed.shape[-1]
    row = lax.broadcasted_iota(jnp.int32, (width, width), 0)
    col = lax.broadcasted_iota(jnp.int32, (width, width), 1)
    start = (index % pairs) * width
    mixed = packed[start : start + width, :]
    turned = mixed.T
    if index < pairs:
        return jnp.where(col >= row, mixed, turned)
    diagonal = side[index - pairs : index - pairs + 1, :]
    return jnp.where(col > row, turned, jnp.where(col == row, diagonal, mixed))


def face_kernel(cross_axes, with_inner, scal_ref, picks_ref, plus_ref, *refs):
    packed_refs = refs[: len(cross_axes)]
    rest = refs[len(cross_axes) :]
    inner_ref = rest[0] if with_inner else None
    rest = rest[1:] if with_inner else rest
    v0_ref = rest[0]
    c_ref, e_ref, m_scr, v_scr, w_scr = rest[-5:]
    if len(rest) > 6:
        c_ref[...] = rest[1][...]
        e_ref[...] = rest[2][...]
    crossing, width = plus_ref.shape[1], plus_ref.shape[-1]
    pairs = crossing // 2
    first = cross_axes[0] * crossing
    own = scal_ref[0]
    f = 0
    for a, packed in zip(cross_axes, packed_refs):
        if len(packed.shape) == 3:
            for k in range(crossing):
                m_scr[f] = own * plus_ref[a, k] + packed[k]
                v_scr[f] = v0_ref[first + f]
                f += 1
            continue
        side = packed[pairs * width :, :]
        next_scale = side[pairs : pairs + 1, 0:1]
        for k in range(crossing):
            m_scr[f] = own * plus_ref[a, k] + next_scale * unpacked(packed, side, k, pairs)
            v_scr[f] = v0_ref[first + f]
            f += 1
    if with_inner:
        for k in range(inner_ref.shape[1]):
            m_scr[f] = own * inner_ref[0, k] + own * inner_ref[1, k]
            v_scr[f] = v0_ref[first + f]
            f += 1
    iterate(own, picks_ref, first, c_ref, e_ref, m_scr, v_scr, w_scr)


def run_faces(kernel, faces, nsel, width, count, smem_args, vmem_args, earlier=()):
    vmem = pltpu.MemorySpace.VMEM
    smem = pltpu.MemorySpace.SMEM
    total = vmem_args[-1].shape[0]
    args = (*smem_args, *vmem_args, *earlier)
    aliases = {len(args) - len(earlier) + i: i for i in range(len(earlier))}
    return pl.pallas_call(
        kernel,
        out_shape=(
            jax.ShapeDtypeStruct((total, nsel, width), jnp.float32),
            jax.ShapeDtypeStruct((total, nsel, nsel), jnp.float32),
        ),
        in_specs=[pl.BlockSpec(memory_space=smem)] * len(smem_args)
        + [pl.BlockSpec(memory_space=vmem)] * (len(vmem_args) + len(earlier)),
        out_specs=(pl.BlockSpec(memory_space=vmem), pl.BlockSpec(memory_space=vmem)),
        scratch_shapes=[
            pltpu.VMEM((faces, width, width), jnp.float32),
            pltpu.VMEM((faces, count, width), jnp.float32),
            pltpu.VMEM((faces, count, width), jnp.float32),
        ],
        input_output_aliases=aliases,
        compiler_params=pltpu.CompilerParams(vmem_limit_bytes=60 * 1024 * 1024),
    )(*args)


def per_device(
    plus_blocks, minus_blocks, inner_blocks, initial_subspace, picks, owner, material_class, coef
):
    plus_local = plus_blocks[0, 0, 0]
    minus_local = minus_blocks[0, 0, 0]
    inner_local = inner_blocks[0, 0, 0]
    basis_vectors = initial_subspace[0, 0, 0]
    picks_flat = picks[0, 0, 0].reshape(-1)
    dims, crossing, width = plus_local.shape[0], plus_local.shape[1], plus_local.shape[-1]
    faces_all, count = basis_vectors.shape[0], basis_vectors.shape[1]
    nsel = picks.shape[-1]
    pairs = crossing // 2
    matches = material_class.reshape(()) == jnp.arange(coef.shape[0], dtype=jnp.int32)
    own_scale = jnp.sum(jnp.where(matches, coef, 0.0))
    row = lax.broadcasted_iota(jnp.int32, (width, width), 0)
    col = lax.broadcasted_iota(jnp.int32, (width, width), 1)
    axes = ("gx", "gy", "gz")
    packed_in = []
    for a in range(dims):
        halves = minus_local[a]
        if a == dims - 1:
            packed_in.append(passed_along(own_scale * halves, axes[a], -1))
            continue
        packed = jnp.where(col >= row, halves[:pairs], halves[pairs:]).reshape(pairs * width, width)
        diagonals = jnp.sum(jnp.where(col == row, halves[pairs:], 0.0), axis=1)
        scale_row = jnp.broadcast_to(own_scale, (1, width))
        pad = jnp.zeros((-(pairs + 1) % 8, width), jnp.float32)
        message = jnp.concatenate([packed, diagonals, scale_row, pad], axis=0)
        packed_in.append(passed_along(message, axes[a], -1))

    scal = own_scale.reshape(1)
    n_inner = inner_local.shape[1]
    late = tuple(range(dims - 1))
    early_c, early_e = run_faces(
        functools.partial(face_kernel, (dims - 1,), True), crossing + n_inner, nsel, width, count,
        (scal, picks_flat), (plus_local, packed_in[dims - 1], inner_local, basis_vectors),
    )
    constraints, blocks = run_faces(
        functools.partial(face_kernel, late, False), len(late) * crossing, nsel, width, count,
        (scal, picks_flat), (plus_local, *packed_in[: dims - 1], basis_vectors), (early_c, early_e),
    )
    flat = blocks.reshape(faces_all, -1)
    groups = lax.axis_size("gz")
    rows_all = groups * CROWS
    owner_hot = (owner[0, 0, 0][:, None] == jnp.arange(rows_all, dtype=jnp.int32)).astype(jnp.float32)
    term = jnp.einsum("fr,fe->re", owner_hot, flat, precision=HIGHEST).reshape(groups, CROWS, -1)
    coarse = jnp.sum(lax.all_to_all(term, "gz", 0, 0), axis=0)
    return (constraints[None, None, None], coarse[None, None])


def solution(mesh):
    return jax.shard_map(
        per_device,
        mesh=mesh,
        in_specs=(
            P("gx", "gy", "gz", None, None, None, None),
            P("gx", "gy", "gz", None, None, None, None),
            P("gx", "gy", "gz", None, None, None, None),
            P("gx", "gy", "gz", None, None, None),
            P("gx", "gy", "gz", None, None),
            P("gx", "gy", "gz", None),
            P("gx", "gy", "gz"),
            P(),
        ),
        out_specs=(P("gx", "gy", "gz", None, None, None), P("gx", "gy", "gz", None)),
        check_vma=False,
    )
```

```python
import functools
import math

import jax
import jax.numpy as jnp
from jax import lax
from jax.experimental import pallas as pl
from jax.experimental.pallas import tpu as pltpu
from jax.sharding import PartitionSpec as P

ITERS = 4
CROWS = 16
HIGHEST = lax.Precision.HIGHEST


def passed_along(block, axis, distance):
    devices = range(lax.axis_size(axis))
    route = [(i - distance, i) for i in devices if i - distance in devices]
    return lax.ppermute(block, axis, route)


GROUP = 8


def eliminate(grams, count):
    state = []
    for gram in grams:
        faces = gram.shape[0] // count
        shape = (faces, count, gram.shape[1])
        face = lax.broadcasted_iota(jnp.int32, shape, 0)
        sub = lax.broadcasted_iota(jnp.int32, shape, 1)
        lane = lax.broadcasted_iota(jnp.int32, shape, 2)
        base = face * count
        left = jnp.where(lane // count == face, gram.reshape(shape), 0.0)
        right = (lane == base + sub).astype(jnp.float32)
        state.append([left, right, sub, lane, base])
    for j in range(count):
        for item in state:
            left, right, sub, lane, base = item
            row_l = jnp.sum(jnp.where(sub == j, left, 0.0), axis=1, keepdims=True)
            row_r = jnp.sum(jnp.where(sub == j, right, 0.0), axis=1, keepdims=True)
            at_pivot = lane == base + j
            pivot = jnp.sum(jnp.where(at_pivot[:, :1], row_l, 0.0), axis=2, keepdims=True)
            inv = 1.0 / jnp.sqrt(pivot)
            col = jnp.sum(jnp.where(at_pivot, left, 0.0), axis=2, keepdims=True) * inv
            col = jnp.where(sub[:, :, :1] > j, col, 0.0)
            row_l = row_l * inv
            row_r = row_r * inv
            item[0] = jnp.where(sub == j, row_l, left - col * row_l)
            item[1] = jnp.where(sub == j, row_r, right - col * row_r)
    return [item[1].reshape(item[1].shape[0] * count, -1) for item in state]


def iterate(own, picks_ref, first, c_ref, e_ref, m_scr, v_scr, w_scr):
    faces, count = v_scr.shape[0], v_scr.shape[1]
    nsel = c_ref.shape[1]
    scale_out = math.sqrt(m_scr.shape[-1])
    spans = [(g, min(g + GROUP, faces)) for g in range(0, faces, GROUP)]

    def image(f, carry):
        w_scr[f] = jnp.dot(v_scr[f], m_scr[f], precision=HIGHEST, preferred_element_type=jnp.float32)
        return carry

    for iteration in range(ITERS):
        lax.fori_loop(0, faces, image, 0, unroll=4)
        images = [w_scr[g0:g1].reshape((g1 - g0) * count, -1) for g0, g1 in spans]
        grams = [
            lax.dot_general(
                w, w, (((1,), (1,)), ((), ())), precision=HIGHEST, preferred_element_type=jnp.float32
            )
            for w in images
        ]
        inverses = eliminate(grams, count)
        for (g0, g1), inverse, w in zip(spans, inverses, images):
            solved = jnp.dot(inverse, w, precision=HIGHEST, preferred_element_type=jnp.float32)
            v_scr[g0:g1] = solved.reshape(g1 - g0, count, -1)

    def finish(f, carry):
        rows = [v_scr[f, pl.ds(picks_ref[(first + f) * nsel + s], 1), :] for s in range(nsel)]
        picked = jnp.concatenate(rows, axis=0)
        c_ref[first + f] = picked * scale_out
        images = jnp.dot(picked, m_scr[f], precision=HIGHEST, preferred_element_type=jnp.float32)
        block = lax.dot_general(
            picked, images, (((1,), (1,)), ((), ())), precision=HIGHEST, preferred_element_type=jnp.float32
        )
        e_ref[first + f] = block / own
        return carry

    lax.fori_loop(0, faces, finish, 0, unroll=2)


def unpacked(packed, side, index, pairs):
    width = packed.shape[-1]
    row = lax.broadcasted_iota(jnp.int32, (width, width), 0)
    col = lax.broadcasted_iota(jnp.int32, (width, width), 1)
    start = (index % pairs) * width
    mixed = packed[start : start + width, :]
    turned = mixed.T
    if index < pairs:
        return jnp.where(col >= row, mixed, turned)
    diagonal = side[index - pairs : index - pairs + 1, :]
    return jnp.where(col > row, turned, jnp.where(col == row, diagonal, mixed))


def face_kernel(cross_axes, with_inner, scal_ref, picks_ref, plus_ref, *refs):
    packed_refs = refs[: len(cross_axes)]
    rest = refs[len(cross_axes) :]
    inner_ref = rest[0] if with_inner else None
    rest = rest[1:] if with_inner else rest
    v0_ref = rest[0]
    c_ref, e_ref, m_scr, v_scr, w_scr = rest[-5:]
    if len(rest) > 6:
        c_ref[...] = rest[1][...]
        e_ref[...] = rest[2][...]
    crossing, width = plus_ref.shape[1], plus_ref.shape[-1]
    pairs = crossing // 2
    first = cross_axes[0] * crossing
    own = scal_ref[0]
    f = 0
    for a, packed in zip(cross_axes, packed_refs):
        side = packed[pairs * width :, :]
        next_scale = side[pairs : pairs + 1, 0:1]
        for k in range(crossing):
            m_scr[f] = own * plus_ref[a - cross_axes[0], k] + next_scale * unpacked(packed, side, k, pairs)
            v_scr[f] = v0_ref[first + f]
            f += 1
    if with_inner:
        for k in range(inner_ref.shape[1]):
            m_scr[f] = own * inner_ref[0, k] + own * inner_ref[1, k]
            v_scr[f] = v0_ref[first + f]
            f += 1
    iterate(own, picks_ref, first, c_ref, e_ref, m_scr, v_scr, w_scr)


def run_faces(kernel, faces, nsel, width, count, smem_args, vmem_args, axes, earlier=()):
    vmem = pltpu.MemorySpace.VMEM
    smem = pltpu.MemorySpace.SMEM
    total = vmem_args[-1].shape[0]
    args = (*smem_args, *vmem_args, *earlier)
    aliases = {len(args) - len(earlier) + i: i for i in range(len(earlier))}
    plus_shape = vmem_args[0].shape
    lowest = axes[0]
    plus_spec = pl.BlockSpec(
        (len(axes),) + plus_shape[1:], lambda i: (lowest // len(axes), 0, 0, 0), memory_space=vmem
    )
    return pl.pallas_call(
        kernel,
        grid=(1,),
        out_shape=(
            jax.ShapeDtypeStruct((total, nsel, width), jnp.float32),
            jax.ShapeDtypeStruct((total, nsel, nsel), jnp.float32),
        ),
        in_specs=[pl.BlockSpec(memory_space=smem)] * len(smem_args)
        + [plus_spec]
        + [pl.BlockSpec(memory_space=vmem)] * (len(vmem_args) - 1 + len(earlier)),
        out_specs=(pl.BlockSpec(memory_space=vmem), pl.BlockSpec(memory_space=vmem)),
        scratch_shapes=[
            pltpu.VMEM((faces, width, width), jnp.float32),
            pltpu.VMEM((faces, count, width), jnp.float32),
            pltpu.VMEM((faces, count, width), jnp.float32),
        ],
        input_output_aliases=aliases,
        compiler_params=pltpu.CompilerParams(vmem_limit_bytes=60 * 1024 * 1024),
    )(*args)


def per_device(
    plus_blocks, minus_blocks, inner_blocks, initial_subspace, picks, owner, material_class, coef
):
    plus_local = plus_blocks[0, 0, 0]
    minus_local = minus_blocks[0, 0, 0]
    inner_local = inner_blocks[0, 0, 0]
    basis_vectors = initial_subspace[0, 0, 0]
    picks_flat = picks[0, 0, 0].reshape(-1)
    dims, crossing, width = plus_local.shape[0], plus_local.shape[1], plus_local.shape[-1]
    faces_all, count = basis_vectors.shape[0], basis_vectors.shape[1]
    nsel = picks.shape[-1]
    pairs = crossing // 2
    matches = material_class.reshape(()) == jnp.arange(coef.shape[0], dtype=jnp.int32)
    own_scale = jnp.sum(jnp.where(matches, coef, 0.0))
    row = lax.broadcasted_iota(jnp.int32, (width, width), 0)
    col = lax.broadcasted_iota(jnp.int32, (width, width), 1)
    axes = ("gx", "gy", "gz")
    packed_in = []
    for a in range(dims):
        halves = minus_local[a]
        packed = jnp.where(col >= row, halves[:pairs], halves[pairs:]).reshape(pairs * width, width)
        diagonals = jnp.sum(jnp.where(col == row, halves[pairs:], 0.0), axis=1)
        scale_row = jnp.broadcast_to(own_scale, (1, width))
        pad = jnp.zeros((-(pairs + 1) % 8, width), jnp.float32)
        message = jnp.concatenate([packed, diagonals, scale_row, pad], axis=0)
        packed_in.append(passed_along(message, axes[a], -1))

    scal = own_scale.reshape(1)
    n_inner = inner_local.shape[1]
    late = tuple(range(dims - 1))
    early_c, early_e = run_faces(
        functools.partial(face_kernel, (dims - 1,), True), crossing + n_inner, nsel, width, count,
        (scal, picks_flat), (plus_local, packed_in[dims - 1], inner_local, basis_vectors), (dims - 1,),
    )
    constraints, blocks = run_faces(
        functools.partial(face_kernel, late, False), len(late) * crossing, nsel, width, count,
        (scal, picks_flat), (plus_local, *packed_in[: dims - 1], basis_vectors), late, (early_c, early_e),
    )
    flat = blocks.reshape(faces_all, -1)
    groups = lax.axis_size("gz")
    rows_all = groups * CROWS
    owner_hot = (owner[0, 0, 0][:, None] == jnp.arange(rows_all, dtype=jnp.int32)).astype(jnp.float32)
    term = jnp.einsum("fr,fe->re", owner_hot, flat, precision=HIGHEST).reshape(groups, CROWS, -1)
    coarse = jnp.sum(lax.all_to_all(term, "gz", 0, 0), axis=0)
    return (constraints[None, None, None], coarse[None, None])


def solution(mesh):
    return jax.shard_map(
        per_device,
        mesh=mesh,
        in_specs=(
            P("gx", "gy", "gz", None, None, None, None),
            P("gx", "gy", "gz", None, None, None, None),
            P("gx", "gy", "gz", None, None, None, None),
            P("gx", "gy", "gz", None, None, None),
            P("gx", "gy", "gz", None, None),
            P("gx", "gy", "gz", None),
            P("gx", "gy", "gz"),
            P(),
        ),
        out_specs=(P("gx", "gy", "gz", None, None, None), P("gx", "gy", "gz", None)),
        check_vma=False,
    )
```

```python
import functools
import math

import jax
import jax.numpy as jnp
from jax import lax
from jax.experimental import pallas as pl
from jax.experimental.pallas import tpu as pltpu
from jax.sharding import PartitionSpec as P

ITERS = 4
CROWS = 16
HIGHEST = lax.Precision.HIGHEST


def passed_along(block, axis, distance):
    devices = range(lax.axis_size(axis))
    route = [(i - distance, i) for i in devices if i - distance in devices]
    return lax.ppermute(block, axis, route)


GROUP = 8


def eliminate(grams, count):
    state = []
    for gram in grams:
        faces = gram.shape[0] // count
        shape = (faces, count, gram.shape[1])
        face = lax.broadcasted_iota(jnp.int32, shape, 0)
        sub = lax.broadcasted_iota(jnp.int32, shape, 1)
        lane = lax.broadcasted_iota(jnp.int32, shape, 2)
        base = face * count
        left = jnp.where(lane // count == face, gram.reshape(shape), 0.0)
        right = (lane == base + sub).astype(jnp.float32)
        state.append([left, right, sub, lane, base])
    for j in range(count):
        for item in state:
            left, right, sub, lane, base = item
            row_l = jnp.sum(jnp.where(sub == j, left, 0.0), axis=1, keepdims=True)
            row_r = jnp.sum(jnp.where(sub == j, right, 0.0), axis=1, keepdims=True)
            at_pivot = lane == base + j
            pivot = jnp.sum(jnp.where(at_pivot[:, :1], row_l, 0.0), axis=2, keepdims=True)
            inv = 1.0 / jnp.sqrt(pivot)
            col = jnp.sum(jnp.where(at_pivot, left, 0.0), axis=2, keepdims=True) * inv
            col = jnp.where(sub[:, :, :1] > j, col, 0.0)
            row_l = row_l * inv
            row_r = row_r * inv
            item[0] = jnp.where(sub == j, row_l, left - col * row_l)
            item[1] = jnp.where(sub == j, row_r, right - col * row_r)
    return [item[1].reshape(item[1].shape[0] * count, -1) for item in state]


def iterate(own, picks_ref, first, c_ref, e_ref, m_scr, v_scr, w_scr):
    faces, count = v_scr.shape[0], v_scr.shape[1]
    nsel = c_ref.shape[1]
    scale_out = math.sqrt(m_scr.shape[-1])
    spans = [(g, min(g + GROUP, faces)) for g in range(0, faces, GROUP)]

    def image(f, carry):
        w_scr[f] = jnp.dot(v_scr[f], m_scr[f], precision=HIGHEST, preferred_element_type=jnp.float32)
        return carry

    for iteration in range(ITERS):
        lax.fori_loop(0, faces, image, 0, unroll=8)
        images = [w_scr[g0:g1].reshape((g1 - g0) * count, -1) for g0, g1 in spans]
        grams = [
            lax.dot_general(
                w, w, (((1,), (1,)), ((), ())), precision=HIGHEST, preferred_element_type=jnp.float32
            )
            for w in images
        ]
        inverses = eliminate(grams, count)
        for (g0, g1), inverse, w in zip(spans, inverses, images):
            solved = jnp.dot(inverse, w, precision=HIGHEST, preferred_element_type=jnp.float32)
            v_scr[g0:g1] = solved.reshape(g1 - g0, count, -1)

    def finish(f, carry):
        rows = [v_scr[f, pl.ds(picks_ref[(first + f) * nsel + s], 1), :] for s in range(nsel)]
        picked = jnp.concatenate(rows, axis=0)
        c_ref[first + f] = picked * scale_out
        images = jnp.dot(picked, m_scr[f], precision=HIGHEST, preferred_element_type=jnp.float32)
        block = lax.dot_general(
            picked, images, (((1,), (1,)), ((), ())), precision=HIGHEST, preferred_element_type=jnp.float32
        )
        e_ref[first + f] = block / own
        return carry

    lax.fori_loop(0, faces, finish, 0, unroll=2)


def unpacked(packed, side, index, pairs):
    width = packed.shape[-1]
    row = lax.broadcasted_iota(jnp.int32, (width, width), 0)
    col = lax.broadcasted_iota(jnp.int32, (width, width), 1)
    start = (index % pairs) * width
    mixed = packed[start : start + width, :]
    turned = mixed.T
    if index < pairs:
        return jnp.where(col >= row, mixed, turned)
    diagonal = side[index - pairs : index - pairs + 1, :]
    return jnp.where(col > row, turned, jnp.where(col == row, diagonal, mixed))


def face_kernel(cross_axes, with_inner, scal_ref, picks_ref, plus_ref, *refs):
    packed_refs = refs[: len(cross_axes)]
    rest = refs[len(cross_axes) :]
    inner_ref = rest[0] if with_inner else None
    rest = rest[1:] if with_inner else rest
    v0_ref = rest[0]
    c_ref, e_ref, m_scr, v_scr, w_scr = rest[-5:]
    if len(rest) > 6:
        c_ref[...] = rest[1][...]
        e_ref[...] = rest[2][...]
    crossing, width = plus_ref.shape[1], plus_ref.shape[-1]
    pairs = crossing // 2
    first = cross_axes[0] * crossing
    own = scal_ref[0]
    f = 0
    for a, packed in zip(cross_axes, packed_refs):
        side = packed[pairs * width :, :]
        next_scale = side[pairs : pairs + 1, 0:1]
        for k in range(crossing):
            m_scr[f] = own * plus_ref[a - cross_axes[0], k] + next_scale * unpacked(packed, side, k, pairs)
            v_scr[f] = v0_ref[first + f]
            f += 1
    if with_inner:
        for k in range(inner_ref.shape[1]):
            m_scr[f] = own * inner_ref[0, k] + own * inner_ref[1, k]
            v_scr[f] = v0_ref[first + f]
            f += 1
    iterate(own, picks_ref, first, c_ref, e_ref, m_scr, v_scr, w_scr)


def run_faces(kernel, faces, nsel, width, count, smem_args, vmem_args, axes, earlier=()):
    vmem = pltpu.MemorySpace.VMEM
    smem = pltpu.MemorySpace.SMEM
    total = vmem_args[-1].shape[0]
    args = (*smem_args, *vmem_args, *earlier)
    aliases = {len(args) - len(earlier) + i: i for i in range(len(earlier))}
    plus_shape = vmem_args[0].shape
    lowest = axes[0]
    plus_spec = pl.BlockSpec(
        (len(axes),) + plus_shape[1:], lambda i: (lowest // len(axes), 0, 0, 0), memory_space=vmem
    )
    return pl.pallas_call(
        kernel,
        grid=(1,),
        out_shape=(
            jax.ShapeDtypeStruct((total, nsel, width), jnp.float32),
            jax.ShapeDtypeStruct((total, nsel, nsel), jnp.float32),
        ),
        in_specs=[pl.BlockSpec(memory_space=smem)] * len(smem_args)
        + [plus_spec]
        + [pl.BlockSpec(memory_space=vmem)] * (len(vmem_args) - 1 + len(earlier)),
        out_specs=(pl.BlockSpec(memory_space=vmem), pl.BlockSpec(memory_space=vmem)),
        scratch_shapes=[
            pltpu.VMEM((faces, width, width), jnp.float32),
            pltpu.VMEM((faces, count, width), jnp.float32),
            pltpu.VMEM((faces, count, width), jnp.float32),
        ],
        input_output_aliases=aliases,
        compiler_params=pltpu.CompilerParams(vmem_limit_bytes=60 * 1024 * 1024),
    )(*args)


def per_device(
    plus_blocks, minus_blocks, inner_blocks, initial_subspace, picks, owner, material_class, coef
):
    plus_local = plus_blocks[0, 0, 0]
    minus_local = minus_blocks[0, 0, 0]
    inner_local = inner_blocks[0, 0, 0]
    basis_vectors = initial_subspace[0, 0, 0]
    picks_flat = picks[0, 0, 0].reshape(-1)
    dims, crossing, width = plus_local.shape[0], plus_local.shape[1], plus_local.shape[-1]
    faces_all, count = basis_vectors.shape[0], basis_vectors.shape[1]
    nsel = picks.shape[-1]
    pairs = crossing // 2
    matches = material_class.reshape(()) == jnp.arange(coef.shape[0], dtype=jnp.int32)
    own_scale = jnp.sum(jnp.where(matches, coef, 0.0))
    row = lax.broadcasted_iota(jnp.int32, (width, width), 0)
    col = lax.broadcasted_iota(jnp.int32, (width, width), 1)
    axes = ("gx", "gy", "gz")
    packed_in = []
    for a in range(dims):
        halves = minus_local[a]
        packed = jnp.where(col >= row, halves[:pairs], halves[pairs:]).reshape(pairs * width, width)
        diagonals = jnp.sum(jnp.where(col == row, halves[pairs:], 0.0), axis=1)
        scale_row = jnp.broadcast_to(own_scale, (1, width))
        pad = jnp.zeros((-(pairs + 1) % 8, width), jnp.float32)
        message = jnp.concatenate([packed, diagonals, scale_row, pad], axis=0)
        packed_in.append(passed_along(message, axes[a], -1))

    scal = own_scale.reshape(1)
    n_inner = inner_local.shape[1]
    late = tuple(range(dims - 1))
    early_c, early_e = run_faces(
        functools.partial(face_kernel, (dims - 1,), True), crossing + n_inner, nsel, width, count,
        (scal, picks_flat), (plus_local, packed_in[dims - 1], inner_local, basis_vectors), (dims - 1,),
    )
    constraints, blocks = run_faces(
        functools.partial(face_kernel, late, False), len(late) * crossing, nsel, width, count,
        (scal, picks_flat), (plus_local, *packed_in[: dims - 1], basis_vectors), late, (early_c, early_e),
    )
    flat = blocks.reshape(faces_all, -1)
    groups = lax.axis_size("gz")
    rows_all = groups * CROWS
    owner_hot = (owner[0, 0, 0][:, None] == jnp.arange(rows_all, dtype=jnp.int32)).astype(jnp.float32)
    term = jnp.einsum("fr,fe->re", owner_hot, flat, precision=HIGHEST).reshape(groups, CROWS, -1)
    coarse = jnp.sum(lax.all_to_all(term, "gz", 0, 0), axis=0)
    return (constraints[None, None, None], coarse[None, None])


def solution(mesh):
    return jax.shard_map(
        per_device,
        mesh=mesh,
        in_specs=(
            P("gx", "gy", "gz", None, None, None, None),
            P("gx", "gy", "gz", None, None, None, None),
            P("gx", "gy", "gz", None, None, None, None),
            P("gx", "gy", "gz", None, None, None),
            P("gx", "gy", "gz", None, None),
            P("gx", "gy", "gz", None),
            P("gx", "gy", "gz"),
            P(),
        ),
        out_specs=(P("gx", "gy", "gz", None, None, None), P("gx", "gy", "gz", None)),
        check_vma=False,
    )
```

```python
import functools
import math

import jax
import jax.numpy as jnp
from jax import lax
from jax.experimental import pallas as pl
from jax.experimental.pallas import tpu as pltpu
from jax.sharding import PartitionSpec as P

ITERS = 4
CROWS = 16
HIGHEST = lax.Precision.HIGHEST


def passed_along(block, axis, distance):
    devices = range(lax.axis_size(axis))
    route = [(i - distance, i) for i in devices if i - distance in devices]
    return lax.ppermute(block, axis, route)


GROUP = 8


def eliminate(grams, count):
    state = []
    for gram in grams:
        faces = gram.shape[0] // count
        shape = (faces, count, gram.shape[1])
        face = lax.broadcasted_iota(jnp.int32, shape, 0)
        sub = lax.broadcasted_iota(jnp.int32, shape, 1)
        lane = lax.broadcasted_iota(jnp.int32, shape, 2)
        base = face * count
        left = jnp.where(lane // count == face, gram.reshape(shape), 0.0)
        right = (lane == base + sub).astype(jnp.float32)
        state.append([left, right, sub, lane, base])
    for j in range(count):
        for item in state:
            left, right, sub, lane, base = item
            row_l = jnp.sum(jnp.where(sub == j, left, 0.0), axis=1, keepdims=True)
            row_r = jnp.sum(jnp.where(sub == j, right, 0.0), axis=1, keepdims=True)
            at_pivot = lane == base + j
            pivot = jnp.sum(jnp.where(at_pivot[:, :1], row_l, 0.0), axis=2, keepdims=True)
            inv = 1.0 / jnp.sqrt(pivot)
            col = jnp.sum(jnp.where(at_pivot, left, 0.0), axis=2, keepdims=True) * inv
            col = jnp.where(sub[:, :, :1] > j, col, 0.0)
            row_l = row_l * inv
            row_r = row_r * inv
            item[0] = jnp.where(sub == j, row_l, left - col * row_l)
            item[1] = jnp.where(sub == j, row_r, right - col * row_r)
    return [item[1].reshape(item[1].shape[0] * count, -1) for item in state]


def iterate(own, picks_ref, first, c_ref, e_ref, m_scr, v_scr, w_scr):
    faces, count = v_scr.shape[0], v_scr.shape[1]
    nsel = c_ref.shape[1]
    scale_out = math.sqrt(m_scr.shape[-1])
    spans = [(g, min(g + GROUP, faces)) for g in range(0, faces, GROUP)]

    def image(f, carry):
        w_scr[f] = jnp.dot(v_scr[f], m_scr[f], precision=HIGHEST, preferred_element_type=jnp.float32)
        return carry

    for iteration in range(ITERS):
        lax.fori_loop(0, faces, image, 0, unroll=8)
        images = [w_scr[g0:g1].reshape((g1 - g0) * count, -1) for g0, g1 in spans]
        grams = [
            lax.dot_general(
                w, w, (((1,), (1,)), ((), ())), precision=HIGHEST, preferred_element_type=jnp.float32
            )
            for w in images
        ]
        inverses = eliminate(grams, count)
        for (g0, g1), inverse, w in zip(spans, inverses, images):
            solved = jnp.dot(inverse, w, precision=HIGHEST, preferred_element_type=jnp.float32)
            v_scr[g0:g1] = solved.reshape(g1 - g0, count, -1)

    def finish(f, carry):
        rows = [v_scr[f, pl.ds(picks_ref[(first + f) * nsel + s], 1), :] for s in range(nsel)]
        picked = jnp.concatenate(rows, axis=0)
        c_ref[first + f] = picked * scale_out
        images = jnp.dot(picked, m_scr[f], precision=HIGHEST, preferred_element_type=jnp.float32)
        block = lax.dot_general(
            picked, images, (((1,), (1,)), ((), ())), precision=HIGHEST, preferred_element_type=jnp.float32
        )
        e_ref[first + f] = block / own
        return carry

    lax.fori_loop(0, faces, finish, 0, unroll=8)


def unpacked(packed, side, index, pairs):
    width = packed.shape[-1]
    row = lax.broadcasted_iota(jnp.int32, (width, width), 0)
    col = lax.broadcasted_iota(jnp.int32, (width, width), 1)
    start = (index % pairs) * width
    mixed = packed[start : start + width, :]
    turned = mixed.T
    if index < pairs:
        return jnp.where(col >= row, mixed, turned)
    diagonal = side[index - pairs : index - pairs + 1, :]
    return jnp.where(col > row, turned, jnp.where(col == row, diagonal, mixed))


def face_kernel(cross_axes, with_inner, scal_ref, picks_ref, plus_ref, *refs):
    packed_refs = refs[: len(cross_axes)]
    rest = refs[len(cross_axes) :]
    inner_ref = rest[0] if with_inner else None
    rest = rest[1:] if with_inner else rest
    v0_ref = rest[0]
    c_ref, e_ref, m_scr, v_scr, w_scr = rest[-5:]
    if len(rest) > 6:
        c_ref[...] = rest[1][...]
        e_ref[...] = rest[2][...]
    crossing, width = plus_ref.shape[1], plus_ref.shape[-1]
    pairs = crossing // 2
    first = cross_axes[0] * crossing
    own = scal_ref[0]
    f = 0
    for a, packed in zip(cross_axes, packed_refs):
        side = packed[pairs * width :, :]
        next_scale = side[pairs : pairs + 1, 0:1]
        for k in range(crossing):
            m_scr[f] = own * plus_ref[a - cross_axes[0], k] + next_scale * unpacked(packed, side, k, pairs)
            v_scr[f] = v0_ref[first + f]
            f += 1
    if with_inner:
        for k in range(inner_ref.shape[1]):
            m_scr[f] = own * inner_ref[0, k] + own * inner_ref[1, k]
            v_scr[f] = v0_ref[first + f]
            f += 1
    iterate(own, picks_ref, first, c_ref, e_ref, m_scr, v_scr, w_scr)


def run_faces(kernel, faces, nsel, width, count, smem_args, vmem_args, axes, earlier=()):
    vmem = pltpu.MemorySpace.VMEM
    smem = pltpu.MemorySpace.SMEM
    total = vmem_args[-1].shape[0]
    args = (*smem_args, *vmem_args, *earlier)
    aliases = {len(args) - len(earlier) + i: i for i in range(len(earlier))}
    plus_shape = vmem_args[0].shape
    lowest = axes[0]
    plus_spec = pl.BlockSpec(
        (len(axes),) + plus_shape[1:], lambda i: (lowest // len(axes), 0, 0, 0), memory_space=vmem
    )
    return pl.pallas_call(
        kernel,
        grid=(1,),
        out_shape=(
            jax.ShapeDtypeStruct((total, nsel, width), jnp.float32),
            jax.ShapeDtypeStruct((total, nsel, nsel), jnp.float32),
        ),
        in_specs=[pl.BlockSpec(memory_space=smem)] * len(smem_args)
        + [plus_spec]
        + [pl.BlockSpec(memory_space=vmem)] * (len(vmem_args) - 1 + len(earlier)),
        out_specs=(pl.BlockSpec(memory_space=vmem), pl.BlockSpec(memory_space=vmem)),
        scratch_shapes=[
            pltpu.VMEM((faces, width, width), jnp.float32),
            pltpu.VMEM((faces, count, width), jnp.float32),
            pltpu.VMEM((faces, count, width), jnp.float32),
        ],
        input_output_aliases=aliases,
        compiler_params=pltpu.CompilerParams(vmem_limit_bytes=60 * 1024 * 1024),
    )(*args)


def per_device(
    plus_blocks, minus_blocks, inner_blocks, initial_subspace, picks, owner, material_class, coef
):
    plus_local = plus_blocks[0, 0, 0]
    minus_local = minus_blocks[0, 0, 0]
    inner_local = inner_blocks[0, 0, 0]
    basis_vectors = initial_subspace[0, 0, 0]
    picks_flat = picks[0, 0, 0].reshape(-1)
    dims, crossing, width = plus_local.shape[0], plus_local.shape[1], plus_local.shape[-1]
    faces_all, count = basis_vectors.shape[0], basis_vectors.shape[1]
    nsel = picks.shape[-1]
    pairs = crossing // 2
    matches = material_class.reshape(()) == jnp.arange(coef.shape[0], dtype=jnp.int32)
    own_scale = jnp.sum(jnp.where(matches, coef, 0.0))
    row = lax.broadcasted_iota(jnp.int32, (width, width), 0)
    col = lax.broadcasted_iota(jnp.int32, (width, width), 1)
    axes = ("gx", "gy", "gz")
    packed_in = []
    for a in range(dims):
        halves = minus_local[a]
        packed = jnp.where(col >= row, halves[:pairs], halves[pairs:]).reshape(pairs * width, width)
        diagonals = jnp.sum(jnp.where(col == row, halves[pairs:], 0.0), axis=1)
        scale_row = jnp.broadcast_to(own_scale, (1, width))
        pad = jnp.zeros((-(pairs + 1) % 8, width), jnp.float32)
        message = jnp.concatenate([packed, diagonals, scale_row, pad], axis=0)
        packed_in.append(passed_along(message, axes[a], -1))

    scal = own_scale.reshape(1)
    n_inner = inner_local.shape[1]
    late = tuple(range(dims - 1))
    early_c, early_e = run_faces(
        functools.partial(face_kernel, (dims - 1,), True), crossing + n_inner, nsel, width, count,
        (scal, picks_flat), (plus_local, packed_in[dims - 1], inner_local, basis_vectors), (dims - 1,),
    )
    constraints, blocks = run_faces(
        functools.partial(face_kernel, late, False), len(late) * crossing, nsel, width, count,
        (scal, picks_flat), (plus_local, *packed_in[: dims - 1], basis_vectors), late, (early_c, early_e),
    )
    flat = blocks.reshape(faces_all, -1)
    groups = lax.axis_size("gz")
    rows_all = groups * CROWS
    owner_hot = (owner[0, 0, 0][:, None] == jnp.arange(rows_all, dtype=jnp.int32)).astype(jnp.float32)
    term = jnp.einsum("fr,fe->re", owner_hot, flat, precision=HIGHEST).reshape(groups, CROWS, -1)
    coarse = jnp.sum(lax.all_to_all(term, "gz", 0, 0), axis=0)
    return (constraints[None, None, None], coarse[None, None])


def solution(mesh):
    return jax.shard_map(
        per_device,
        mesh=mesh,
        in_specs=(
            P("gx", "gy", "gz", None, None, None, None),
            P("gx", "gy", "gz", None, None, None, None),
            P("gx", "gy", "gz", None, None, None, None),
            P("gx", "gy", "gz", None, None, None),
            P("gx", "gy", "gz", None, None),
            P("gx", "gy", "gz", None),
            P("gx", "gy", "gz"),
            P(),
        ),
        out_specs=(P("gx", "gy", "gz", None, None, None), P("gx", "gy", "gz", None)),
        check_vma=False,
    )
```
